32 devices in a mesh: dp: 4 (over y, x), expert: 8 (over z, core).
Axes of the slice: x: 2, y: 2, z: 4, core: 2. Of those that a mesh axis runs over, the one named last changes fastest.
Arguments:
- tokens: bfloat16 [8, 512, 2048], P('expert', 'dp'), may hold values from -6 to 6
- segment_ids: int32 [8, 512], P('expert', 'dp'), may hold values from 0 to 2, never falling along the last dimension, each value on 1 to 256 neighbouring positions
- routes: int32 [8, 512, 6], P('expert', 'dp'), may hold values from 0 to 15, all different within a row; in each aligned block of 128 rows (0 to 127, 128 to 255, ..., all dimensions but the last counted through in order) at most 64 rows name the same one
- norm_gain: float32 [2048], replicated, may hold values from 0.25 to 1.75
- w_query: bfloat16 [2048, 2048], P(None, 'dp')
- w_key: bfloat16 [2048, 512], P(None, 'dp')
- w_value: bfloat16 [2048, 512], P(None, 'dp'), may hold values from -0.125 to 0.125
- w_out: bfloat16 [2048, 2048], P('dp'), may hold values from -0.125 to 0.125
- ffn_gain: float32 [2048], replicated, may hold values from 0.25 to 1.75
- w_router: bfloat16 [2048, 16], replicated, may hold values from -0.125 to 0.125
- w_shared_gate: bfloat16 [2048, 2816], P(None, 'dp'), may hold values from -0.125 to 0.125
- w_shared_up: bfloat16 [2048, 2816], P(None, 'dp'), may hold values from -0.125 to 0.125
- w_shared_down: bfloat16 [2816, 2048], P('dp'), may hold values from -0.109375 to 0.109375
- w_expert_gate: bfloat16 [2048, 22528], P(None, ('dp', 'expert')), may hold values from -0.125 to 0.125
- w_expert_up: bfloat16 [2048, 22528], P(None, ('dp', 'expert')), may hold values from -0.125 to 0.125
- w_expert_down: bfloat16 [22528, 2048], P(('dp', 'expert')), may hold values from -0.15625 to 0.15625
Outputs:
- layer_out: bfloat16 [8, 512, 2048], P('expert', 'dp')
The draws below stay inside these ranges and needn't reach their ends.
Inputs may be any that keep to these rules, and one draw needn't show every extreme that they name: `routes`: each row names 6 different experts. In each aligned block of 128 rows (stream-major order; the rows of one device) no expert is named more than 64 times, a bound that some block reaches. `segment_ids`: along each stream ids never fall; each of the 3 prompts covers 1 to 256 tokens, one exactly 256.
All inputs are finite; a program needn't handle non-finite values.
Results may differ from the reference program's by a relative error of at most 0.02.
The reference program's roundings to bfloat16 on the way count: a program that leaves them out, or rounds other values in their place, can miss the bound.
Values may be sent and summed in bfloat16 or wider, within the bound.
No kernel may reach another device: no remote copies, remote signals or barrier semaphores. Data moves between devices by JAX's collectives and lax.ppermute only.
A program may use at most 128 MiB of HBM per device.

```python
import math
import jax
import jax.numpy as jnp
import numpy as np
from jax import lax

D = 2048
HEADS = 16
KVH = 4
HD = 128
FFE = 1408
SFF = 2816
TOP = 6
TOK_DEV = 128
SEGS = 3
STREAMS = 8
GROUP = 512
SEG_MOST = 256
EXPERTS = 16
CAP = 64
N_DP = 4


def projection(key, heads):
    base = jax.random.truncated_normal(key, -6.0, 6.0, (D, heads * HD), jnp.float32) * D ** (-0.5)
    return base.astype(jnp.bfloat16)


def draw_w_query(key, part):
    return projection(jax.random.fold_in(key, 11), HEADS)


def draw_w_key(key, part):
    return projection(jax.random.fold_in(key, 13), KVH)


def levels(own_key, shape, pieces, low, high):
    factor_of, own = 1.0, jax.random.fold_in(own_key, 6)
    for position, blocks in pieces:
        steps = jnp.exp(jax.random.uniform(jax.random.fold_in(own, position), (blocks,), jnp.float32, low / len(pieces), high / len(pieces)))
        factor_of = factor_of * jnp.repeat(steps, shape[position] // blocks).reshape([-1 if axis == position else 1 for axis in range(len(shape))])
    return factor_of


def profile(amount, total, reach, skew):
    loads = [(1 << 20) // math.isqrt(standing ** skew) + 1 for standing in range(2, amount + 1)]
    surplus, counts = total - reach - (amount - 1), [1] * (amount - 1)
    while surplus > 0:
        free = [i for i in range(amount - 1) if counts[i] < reach]
        mass, left = sum([loads[i] for i in free]), surplus
        for i in free:
            more = min(reach - counts[i], max(1, left * loads[i] // mass), surplus)
            counts[i] = counts[i] + more
            surplus = surplus - more
    return np.array([reach] + counts)


def uneven(key, count, total, most, lean):
    if count == 2:
        one = jax.random.randint(key, (), max(1, total - most), min(most, total - 1) + 1)
        return jnp.stack([one, total - one])
    sizes = jnp.asarray(profile(count, total, most, lean), jnp.int32)
    couples = (count - 1) // 2
    giver, taker = sizes[1:1 + 2 * couples:2], sizes[2:2 + 2 * couples:2]
    margin = jnp.minimum(giver - 1, most - taker)
    passed = jax.random.randint(jax.random.fold_in(key, 1), (couples,), 0, 1 << 20) % (margin + 1)
    sizes = sizes.at[1:1 + 2 * couples:2].set(giver - passed).at[2:2 + 2 * couples:2].set(taker + passed)
    return sizes[jax.random.permutation(jax.random.fold_in(key, 2), count)]


def deal_out(rng, own, number, rows, count, top, bound, lean):
    order = jax.random.permutation(rng, count)
    heavy_load, ordinary = load_shares(count, rows * top, bound, lean, True), load_shares(count, rows * top, bound, lean, False)
    places = jnp.arange(count)

    def named(tallies, offset_by):
        used = int((tallies > 0).sum())
        fixed = max(1, used // 4)
        moved = fixed + (places - fixed + offset_by * (used - fixed)) % max(1, count - fixed)
        return jnp.zeros((count,), jnp.int32).at[order[jnp.where(places < fixed, places, moved)]].set(jnp.asarray(tallies, jnp.int32))

    tallies = jnp.where(number % 4 == 0, named(heavy_load, number // 4), named(ordinary, number - number // 4 - 1))
    mixed = jax.random.permutation(jax.random.fold_in(own, 3), count)
    donor, sink = mixed[0:count // 2 * 2:2], mixed[1:count // 2 * 2:2]
    slack = jnp.minimum(tallies[donor] - 1, bound - tallies[sink]) // 2
    slack = jnp.where((donor == order[0]) | (sink == order[0]) | (tallies[sink] == 0), 0, jnp.maximum(slack, 0))
    moved = jax.random.randint(jax.random.fold_in(own, 4), (count // 2,), 0, 1 << 20) % (slack + 1)
    tallies = tallies.at[donor].add(-moved).at[sink].add(moved)
    labels = jnp.searchsorted(jnp.cumsum(tallies), jnp.arange(rows * top), side="right").astype(jnp.int32)
    table = labels.reshape(top, rows).T
    table = table[jax.random.permutation(jax.random.fold_in(own, 1), rows)]
    offset_by = jax.random.randint(jax.random.fold_in(own, 2), (rows, 1), 0, top)
    return jnp.take_along_axis(table, (jnp.arange(top)[None, :] + offset_by) % top, axis=1)


def load_shares(count, total, most, lean, full):
    portions = [(1 << 20) // math.isqrt(rank ** lean) + 1 for rank in range(1, count + 1)]
    largest = most if full else min(most, max(-(-total // count), total * portions[0] // sum(portions)))
    least = 1 if total - largest >= count - 1 else 0
    given, spare = [largest] + [least] * (count - 1), total - largest - least * (count - 1)
    while spare > 0:
        free = [i for i in range(1, count) if given[i] < largest] or [i for i in range(1, count) if given[i] < most]
        whole, remaining = sum([portions[i] for i in free]), spare
        for i in free:
            extra = min(most - given[i], max(1, remaining * portions[i] // whole), spare)
            given[i] = given[i] + extra
            spare = spare - extra
    return np.array(given)


def centred(rng, shape, scale, reach, cuts=(), kind=jnp.bfloat16):
    array = jax.random.normal(rng, shape, jnp.float32) * scale
    if len(cuts) > 0:
        array = levels(rng, shape, cuts, -0.22, 0.18) * array
    return jnp.clip(array, min=-reach, max=reach).astype(kind)


def setup_inputs(seed: int = 0) -> dict:
    key_of = jax.random.split(jax.random.key(seed), 17)
    tokens = centred(key_of[0], (STREAMS, GROUP, D), 1.0, 6.0, ((0, 8), (1, 4)))
    segment_ids = jax.vmap(lambda own: jnp.searchsorted(jnp.cumsum(uneven(own, SEGS, GROUP, SEG_MOST, 2)), jnp.arange(GROUP), side="right"))(jax.random.split(key_of[1], STREAMS)).reshape((STREAMS, GROUP)).astype(jnp.int32)
    routes_keys = jax.random.split(jax.random.fold_in(key_of[2], 1), STREAMS * GROUP // TOK_DEV)
    routes_turns = jax.random.permutation(jax.random.fold_in(key_of[2], 3), STREAMS * GROUP // TOK_DEV)
    routes = jax.vmap(lambda own, number: deal_out(jax.random.fold_in(key_of[2], 2), own, number, TOK_DEV, EXPERTS, TOP, CAP, 1))(routes_keys, routes_turns).reshape((STREAMS, GROUP, TOP))
    norm_gain = jnp.clip(1.0 + 0.15 * jax.random.normal(key_of[3], (D,), jnp.float32), 0.25, 1.75)
    w_query = draw_w_query(jax.random.fold_in(key_of[16], 71), 0)
    w_key = draw_w_key(jax.random.fold_in(key_of[16], 71), 0)
    w_value = centred(key_of[6], (D, KVH * HD), D ** -0.5, 0.125, ((1, 4),))
    w_out = centred(key_of[7], (HEADS * HD, D), (HEADS * HD) ** -0.5, 0.125, ((0, 4),))
    ffn_gain = jnp.clip(1.0 + 0.15 * jax.random.normal(key_of[8], (D,), jnp.float32), 0.25, 1.75)
    w_router = centred(key_of[9], (D, EXPERTS), D ** -0.5, 0.125)
    w_shared_gate = centred(key_of[10], (D, SFF), D ** -0.5, 0.125, ((1, 4),))
    w_shared_up = centred(key_of[11], (D, SFF), D ** -0.5, 0.125, ((1, 4),))
    w_shared_down = centred(key_of[12], (SFF, D), SFF ** -0.5, 0.109375, ((0, 4),))
    w_expert_gate = centred(key_of[13], (D, EXPERTS * FFE), D ** -0.5, 0.125, ((1, 32),))
    w_expert_up = centred(key_of[14], (D, EXPERTS * FFE), D ** -0.5, 0.125, ((1, 32),))
    w_expert_down = centred(key_of[15], (EXPERTS * FFE, D), FFE ** -0.5, 0.15625, ((0, 32),))
    return {"tokens": tokens, "segment_ids": segment_ids, "routes": routes, "norm_gain": norm_gain, "w_query": w_query, "w_key": w_key, "w_value": w_value, "w_out": w_out, "ffn_gain": ffn_gain, "w_router": w_router, "w_shared_gate": w_shared_gate, "w_shared_up": w_shared_up, "w_shared_down": w_shared_down, "w_expert_gate": w_expert_gate, "w_expert_up": w_expert_up, "w_expert_down": w_expert_down}


epsilon = 1e-06

def rms_norm(values, gain):
    wide = values.astype(jnp.float32)
    scale = lax.rsqrt(lax.optimization_barrier(jnp.mean(wide * wide, axis=-1, keepdims=True)) + epsilon)
    return (wide * scale * gain.astype(jnp.float32)).astype(jnp.bfloat16)

def positions(segment):
    count = segment.shape[0]
    index = jnp.arange(count, dtype=jnp.int32)
    same = (segment[:, None] == segment[None, :]) & (index[None, :] < index[:, None])
    return lax.optimization_barrier(jnp.sum(same.astype(jnp.int32), axis=1))

def rotate(heads, place):
    half = heads.shape[-1] // 2
    freq = 10000.0 ** (-jnp.arange(half, dtype=jnp.float32) / half)
    angle = place.astype(jnp.float32)[:, None] * freq[None, :]
    cosine = jnp.cos(angle)[:, None, :]
    sine = jnp.sin(angle)[:, None, :]
    first = heads[..., :half]
    second = heads[..., half:]
    return jnp.concatenate([first * cosine - second * sine, second * cosine + first * sine], axis=-1)

def attend(normed, segment, w_query, w_key, w_value):
    rows = normed.shape[0]
    query_heads = w_query.shape[1] // HD
    value_heads = w_key.shape[1] // HD
    group_size = query_heads // value_heads
    place = positions(segment)
    query = jnp.dot(normed, w_query, preferred_element_type=jnp.float32).reshape(rows, query_heads, HD)
    query = rotate(query, place).astype(jnp.bfloat16).reshape(rows, value_heads, group_size, HD)
    keyed = jnp.dot(normed, w_key, preferred_element_type=jnp.float32).reshape(rows, value_heads, HD)
    keyed = rotate(keyed, place).astype(jnp.bfloat16)
    valued = jnp.dot(normed, w_value, preferred_element_type=jnp.float32).astype(jnp.bfloat16).reshape(rows, value_heads, HD)
    block = min(rows, 512)
    index = jnp.arange(rows, dtype=jnp.int32)

    def one_block(start):
        query_block = lax.dynamic_slice_in_dim(query, start, block, 0)
        segment_block = lax.dynamic_slice_in_dim(segment, start, block, 0)
        index_block = start + jnp.arange(block, dtype=jnp.int32)
        scores = jnp.einsum('qkgd,skd->kgqs', query_block.astype(jnp.float32), keyed.astype(jnp.float32)) * HD ** (-0.5)
        allowed = (segment_block[:, None] == segment[None, :]) & (index[None, :] <= index_block[:, None])
        scores = jnp.where(allowed[None, None], scores, -1e+30)
        highest = lax.optimization_barrier(jnp.max(scores, axis=-1, keepdims=True))
        expo = jnp.exp(scores - highest)
        weights = (expo / lax.optimization_barrier(jnp.sum(expo, axis=-1, keepdims=True))).astype(jnp.bfloat16)
        mixed = jnp.einsum('kgqs,skd->qkgd', weights.astype(jnp.float32), valued.astype(jnp.float32))
        return mixed.astype(jnp.bfloat16).reshape(block, query_heads * HD)
    starts = jnp.arange(rows // block, dtype=jnp.int32) * block
    return lax.map(one_block, starts).reshape(rows, query_heads * HD)

def rounded(values):
    return lax.optimization_barrier(values.astype(jnp.bfloat16)).astype(jnp.float32)

def route_gates(logits, route):
    chosen = jnp.take_along_axis(logits, route, axis=1)
    highest = lax.optimization_barrier(jnp.max(chosen, axis=1, keepdims=True))
    expo = jnp.exp(chosen - highest)
    return expo / lax.optimization_barrier(jnp.sum(expo, axis=1, keepdims=True))

def reference(tokens, segment_ids, routes, norm_gain, w_query, w_key, w_value, w_out, ffn_gain, w_router, w_shared_gate, w_shared_up, w_shared_down, w_expert_gate, w_expert_up, w_expert_down):
    width = tokens.shape[2]
    head_width = w_out.shape[0] // N_DP
    shared_width = w_shared_down.shape[0] // N_DP
    expert_count = w_router.shape[1]

    def stream_part(inputs):
        rows, segment, route = inputs
        normed = rms_norm(rows, norm_gain)
        attended = attend(normed, segment, w_query, w_key, w_value)
        head_sum = jnp.zeros((rows.shape[0], width), jnp.float32)
        for block in range(N_DP):
            part = jnp.dot(attended[:, block * head_width:(block + 1) * head_width], w_out[block * head_width:(block + 1) * head_width], preferred_element_type=jnp.float32)
            head_sum = head_sum + rounded(part)
        residual = (rows.astype(jnp.float32) + head_sum).astype(jnp.bfloat16)
        mixed = rms_norm(residual, ffn_gain)
        hidden = (jax.nn.silu(jnp.dot(mixed, w_shared_gate, preferred_element_type=jnp.float32)) * jnp.dot(mixed, w_shared_up, preferred_element_type=jnp.float32)).astype(jnp.bfloat16)
        shared_sum = jnp.zeros((rows.shape[0], width), jnp.float32)
        for block in range(N_DP):
            part = jnp.dot(hidden[:, block * shared_width:(block + 1) * shared_width], w_shared_down[block * shared_width:(block + 1) * shared_width], preferred_element_type=jnp.float32)
            shared_sum = shared_sum + rounded(part)
        logits = jnp.dot(mixed, w_router, preferred_element_type=jnp.float32)
        gates = route_gates(logits, route)
        return (residual, shared_sum, mixed, gates)
    residual, shared_sum, mixed, gates = lax.map(stream_part, (tokens, segment_ids, routes))
    total_tokens = tokens.shape[0] * tokens.shape[1]
    blocks = total_tokens // TOK_DEV
    capacity = 4 * TOK_DEV * TOP // (3 * expert_count)
    total_routes = total_tokens * TOP
    flat_routes = routes.reshape(blocks, TOK_DEV * TOP)
    onehot = (flat_routes[:, :, None] == jnp.arange(expert_count, dtype=jnp.int32)[None, None, :]).astype(jnp.int32)
    slot = lax.optimization_barrier(jnp.sum(jnp.cumsum(onehot, axis=1) * onehot, axis=2)) - 1
    route_id = jnp.arange(total_routes, dtype=jnp.int32).reshape(blocks, TOK_DEV * TOP)
    block_id = jnp.broadcast_to(jnp.arange(blocks, dtype=jnp.int32)[:, None], (blocks, TOK_DEV * TOP))
    table = jnp.full((expert_count, blocks, capacity), total_routes, jnp.int32).at[flat_routes, block_id, slot].set(route_id)
    mixed_flat = mixed.reshape(total_tokens, width)
    gates_flat = gates.reshape(total_routes)
    half = FFE // 2

    def expert_step(carry, expert):
        ids = table[expert].reshape(-1)
        valid = ids < total_routes
        safe = jnp.where(valid, ids, 0)
        token = safe // TOP
        rows = jnp.where(valid[:, None], mixed_flat[token], jnp.zeros((), jnp.bfloat16)).astype(jnp.bfloat16)
        total = jnp.zeros((rows.shape[0], width), jnp.float32)
        for side in range(2):
            column = (expert * FFE + side * half).astype(jnp.int32)
            gate_cols = lax.dynamic_slice_in_dim(w_expert_gate, column, half, 1)
            up_cols = lax.dynamic_slice_in_dim(w_expert_up, column, half, 1)
            down_rows = lax.dynamic_slice_in_dim(w_expert_down, column, half, 0)
            active = (jax.nn.silu(jnp.dot(rows, gate_cols, preferred_element_type=jnp.float32)) * jnp.dot(rows, up_cols, preferred_element_type=jnp.float32)).astype(jnp.bfloat16)
            total = total + rounded(jnp.dot(active, down_rows, preferred_element_type=jnp.float32))
        output = rounded(total)
        term = jnp.where(valid[:, None], gates_flat[safe][:, None] * output, 0.0)
        return (carry.at[token].add(term), None)
    routed, unused = lax.scan(expert_step, jnp.zeros((total_tokens, width), jnp.float32), jnp.arange(expert_count, dtype=jnp.int32))
    routed = routed.reshape(tokens.shape)
    return (residual.astype(jnp.float32) + shared_sum + routed).astype(jnp.bfloat16)
```

```python
import jax
import jax.numpy as jnp
from jax import lax
from jax.sharding import PartitionSpec as P

HD = 128
TOP = 6


epsilon = 1e-06


def rms_norm(values, gain):
    wide = values.astype(jnp.float32)
    scale = lax.rsqrt(jnp.mean(wide * wide, axis=-1, keepdims=True) + epsilon)
    return (wide * scale * gain).astype(jnp.bfloat16)


def positions(segment):
    count = segment.shape[0]
    index = jnp.arange(count, dtype=jnp.int32)
    same = (segment[:, None] == segment[None, :]) & (index[None, :] < index[:, None])
    return jnp.sum(same.astype(jnp.int32), axis=1)


def rotate(heads, place):
    half = heads.shape[-1] // 2
    freq = 10000.0 ** (-jnp.arange(half, dtype=jnp.float32) / half)
    angle = place.astype(jnp.float32)[:, None] * freq[None, :]
    cosine = jnp.cos(angle)[:, None, :]
    sine = jnp.sin(angle)[:, None, :]
    first = heads[..., :half]
    second = heads[..., half:]
    return jnp.concatenate(
        [first * cosine - second * sine, second * cosine + first * sine], axis=-1
    )


def attend(normed, segment, w_query, w_key, w_value):
    rows = normed.shape[0]
    query_heads = w_query.shape[1] // HD
    value_heads = w_key.shape[1] // HD
    group_size = query_heads // value_heads
    place = positions(segment)
    query = jnp.dot(normed, w_query, preferred_element_type=jnp.float32).reshape(
        rows, query_heads, HD
    )
    query = rotate(query, place).astype(jnp.bfloat16).reshape(rows, value_heads, group_size, HD)
    keyed = jnp.dot(normed, w_key, preferred_element_type=jnp.float32).reshape(
        rows, value_heads, HD
    )
    keyed = rotate(keyed, place).astype(jnp.bfloat16)
    valued = (
        jnp.dot(normed, w_value, preferred_element_type=jnp.float32)
        .astype(jnp.bfloat16)
        .reshape(rows, value_heads, HD)
    )
    block = min(rows, 512)
    index = jnp.arange(rows, dtype=jnp.int32)

    def one_block(start):
        index_block = start + jnp.arange(block, dtype=jnp.int32)
        scores = jnp.einsum(
            "qkgd,skd->kgqs", query, keyed, preferred_element_type=jnp.float32
        ) * HD ** (-0.5)
        allowed = (segment[:, None] == segment[None, :]) & (index[None, :] <= index_block[:, None])
        scores = jnp.where(allowed[None, None], scores, -1e30)
        highest = jnp.max(scores, axis=-1, keepdims=True)
        expo = jnp.exp(scores - highest)
        weights = (expo / jnp.sum(expo, axis=-1, keepdims=True)).astype(jnp.bfloat16)
        mixed = jnp.einsum("kgqs,skd->qkgd", weights, valued, preferred_element_type=jnp.float32)
        return mixed.astype(jnp.bfloat16).reshape(block, query_heads * HD)

    starts = jnp.arange(rows // block, dtype=jnp.int32) * block
    return lax.map(one_block, starts).reshape(rows, query_heads * HD)


def expert_rows(rows, w_expert_gate, w_expert_up, w_expert_down):
    shape = rows.shape
    flat = rows.reshape(-1, shape[-1])
    gated = jnp.dot(flat, w_expert_gate, preferred_element_type=jnp.float32)
    lifted = jnp.dot(flat, w_expert_up, preferred_element_type=jnp.float32)
    active = (jax.nn.silu(gated) * lifted).astype(jnp.bfloat16)
    return (
        jnp.dot(active, w_expert_down, preferred_element_type=jnp.float32)
        .astype(jnp.bfloat16)
        .reshape(shape)
    )


def per_device(
    tokens,
    segment_ids,
    routes,
    norm_gain,
    w_query,
    w_key,
    w_value,
    w_out,
    ffn_gain,
    w_router,
    w_shared_gate,
    w_shared_up,
    w_shared_down,
    w_expert_gate,
    w_expert_up,
    w_expert_down,
):
    own_rows = tokens[0]
    tok_count = own_rows.shape[0]
    width = own_rows.shape[1]
    normed = rms_norm(own_rows, norm_gain)
    group_rows, group_segments = (
        lax.all_gather(normed, "dp", axis=0, tiled=True),
        lax.all_gather(segment_ids[0], "dp", axis=0, tiled=True),
    )
    attended = attend(group_rows, group_segments, w_query, w_key, w_value)
    head_sum = lax.psum_scatter(
        jnp.dot(attended, w_out, preferred_element_type=jnp.float32).astype(jnp.bfloat16),
        "dp",
        scatter_dimension=0,
        tiled=True,
    ).astype(jnp.float32)
    residual = (own_rows.astype(jnp.float32) + head_sum).astype(jnp.bfloat16)
    mixed = rms_norm(residual, ffn_gain)
    piece = lax.all_gather(mixed, "dp", axis=0, tiled=True)
    gated = jnp.dot(piece, w_shared_gate, preferred_element_type=jnp.float32)
    lifted = jnp.dot(piece, w_shared_up, preferred_element_type=jnp.float32)
    hidden = (jax.nn.silu(gated) * lifted).astype(jnp.bfloat16)
    shared_sum = lax.psum_scatter(
        jnp.dot(hidden, w_shared_down, preferred_element_type=jnp.float32).astype(jnp.bfloat16),
        "dp",
        scatter_dimension=0,
        tiled=True,
    ).astype(jnp.float32)
    expert_count = w_router.shape[1]
    dp_size = lax.axis_size("dp")
    planes = lax.axis_size("zc")
    plane = lax.axis_index("zc")
    capacity = 4 * tok_count * TOP // (3 * expert_count)
    depth = planes * capacity
    slots = dp_size * depth
    mixed_g = lax.all_gather(mixed, "zc", axis=0, tiled=True)
    routes_g = lax.all_gather(routes[0], "zc", axis=0, tiled=True)
    rows_g = mixed_g.shape[0]
    labels = jnp.arange(expert_count, dtype=jnp.int32)
    logits = jnp.dot(mixed_g, w_router, preferred_element_type=jnp.float32)
    chosen = jnp.sum(
        jnp.where(routes_g[:, :, None] == labels[None, None, :], logits[:, None, :], 0.0), axis=2
    )
    highest = jnp.max(chosen, axis=1, keepdims=True)
    expo = jnp.exp(chosen - highest)
    gates = expo / jnp.sum(expo, axis=1, keepdims=True)
    route_flat = routes_g.reshape(-1)
    inside = (route_flat % planes) == plane
    dest = route_flat // planes
    onehot = ((dest[:, None] == jnp.arange(dp_size, dtype=jnp.int32)[None, :]) & inside[:, None]).astype(jnp.int32)
    slot = jnp.sum(jnp.cumsum(onehot, axis=0) * onehot, axis=1) - 1
    target = jnp.where(inside, dest * depth + slot, -1).reshape(rows_g, TOP)
    hit = target[:, :, None] == jnp.arange(slots, dtype=jnp.int32)[None, None, :]
    placed = jnp.any(hit, axis=1).astype(jnp.bfloat16)
    send = lax.dot_general(
        placed, mixed_g, (((0,), (0,)), ((), ())), preferred_element_type=jnp.float32
    ).astype(jnp.bfloat16)
    recv = lax.all_to_all(send.reshape(dp_size, depth, width), "dp", 0, 0, tiled=True)
    mine = recv.reshape(slots, width)
    swap = [(0, 1), (1, 0)]
    other = lax.ppermute(mine, "core", swap)
    half_rows = expert_rows(
        jnp.concatenate([mine, other], axis=0), w_expert_gate, w_expert_up, w_expert_down
    )
    from_partner = lax.ppermute(half_rows[slots:], "core", swap)
    expert_out = (
        half_rows[:slots].astype(jnp.float32) + from_partner.astype(jnp.float32)
    ).astype(jnp.bfloat16)
    back = lax.all_to_all(
        expert_out.reshape(dp_size, depth, width), "dp", 0, 0, tiled=True
    ).reshape(slots, width)
    comb = jnp.sum(jnp.where(hit, gates[:, :, None], 0.0), axis=1)
    first = comb.astype(jnp.bfloat16)
    rest = comb - first.astype(jnp.float32)
    second = rest.astype(jnp.bfloat16)
    third = (rest - second.astype(jnp.float32)).astype(jnp.bfloat16)
    partial = (
        jnp.dot(first, back, preferred_element_type=jnp.float32)
        + jnp.dot(second, back, preferred_element_type=jnp.float32)
        + jnp.dot(third, back, preferred_element_type=jnp.float32)
    )
    routed = lax.psum_scatter(
        partial.astype(jnp.bfloat16), "zc", scatter_dimension=0, tiled=True
    ).astype(jnp.float32)
    output = (residual.astype(jnp.float32) + shared_sum + routed).astype(jnp.bfloat16)
    return output[None]


def solution(mesh):
    dp_size = mesh.shape["dp"]
    planes = mesh.shape["expert"] // 2
    fine = jax.sharding.Mesh(mesh.devices.reshape(dp_size, planes, 2), ("dp", "zc", "core"))
    ex = ("zc", "core")
    in_specs = (
        P(ex, "dp", None),
        P(ex, "dp"),
        P(ex, "dp", None),
        P(),
        P(None, "dp"),
        P(None, "dp"),
        P(None, "dp"),
        P("dp", None),
        P(),
        P(),
        P(None, "dp"),
        P(None, "dp"),
        P("dp", None),
        P(None, ("dp",) + ex),
        P(None, ("dp",) + ex),
        P(("dp",) + ex, None),
    )
    out_specs = P(ex, "dp", None)
    return jax.shard_map(
        per_device, mesh=fine, in_specs=in_specs, out_specs=out_specs, check_vma=False
    )
```

```python
import jax
import jax.numpy as jnp
from jax import lax
from jax.sharding import PartitionSpec as P

HD = 128
TOP = 6


epsilon = 1e-06


def shifted(x, axis, n, s):
    return lax.ppermute(x, axis, [(i, (i + s) % n) for i in range(n)])


def gather_ring(x, axis):
    n = lax.axis_size(axis)
    me = lax.axis_index(axis)
    parts = [x] + [shifted(x, axis, n, s) for s in range(1, n)]
    order = (me - jnp.arange(n, dtype=jnp.int32)) % n
    stacked = jnp.take(jnp.stack(parts), order, axis=0)
    return stacked.reshape((n * x.shape[0],) + x.shape[1:])


def scatter_sum(x, axis):
    n = lax.axis_size(axis)
    me = lax.axis_index(axis)
    blocks = x.reshape((n, x.shape[0] // n) + x.shape[1:])
    total = blocks[me].astype(jnp.float32)
    for s in range(1, n):
        total = total + shifted(blocks[(me + s) % n], axis, n, s).astype(jnp.float32)
    return total


def exchange(x, axis):
    n = lax.axis_size(axis)
    me = lax.axis_index(axis)
    got = [x[me]] + [shifted(x[(me + s) % n], axis, n, s) for s in range(1, n)]
    order = (me - jnp.arange(n, dtype=jnp.int32)) % n
    return jnp.take(jnp.stack(got), order, axis=0)


def rms_norm(values, gain):
    wide = values.astype(jnp.float32)
    scale = lax.rsqrt(jnp.mean(wide * wide, axis=-1, keepdims=True) + epsilon)
    return (wide * scale * gain).astype(jnp.bfloat16)


def positions(segment):
    count = segment.shape[0]
    index = jnp.arange(count, dtype=jnp.int32)
    same = (segment[:, None] == segment[None, :]) & (index[None, :] < index[:, None])
    return jnp.sum(same.astype(jnp.int32), axis=1)


def rotate(heads, place):
    half = heads.shape[-1] // 2
    freq = 10000.0 ** (-jnp.arange(half, dtype=jnp.float32) / half)
    angle = place.astype(jnp.float32)[:, None] * freq[None, :]
    cosine = jnp.cos(angle)[:, None, :]
    sine = jnp.sin(angle)[:, None, :]
    first = heads[..., :half]
    second = heads[..., half:]
    return jnp.concatenate(
        [first * cosine - second * sine, second * cosine + first * sine], axis=-1
    )


def attend(normed, segment, w_query, w_key, w_value):
    rows = normed.shape[0]
    query_heads = w_query.shape[1] // HD
    value_heads = w_key.shape[1] // HD
    group_size = query_heads // value_heads
    place = positions(segment)
    query = jnp.dot(normed, w_query, preferred_element_type=jnp.float32).reshape(
        rows, query_heads, HD
    )
    query = rotate(query, place).astype(jnp.bfloat16).reshape(rows, value_heads, group_size, HD)
    keyed = jnp.dot(normed, w_key, preferred_element_type=jnp.float32).reshape(
        rows, value_heads, HD
    )
    keyed = rotate(keyed, place).astype(jnp.bfloat16)
    valued = (
        jnp.dot(normed, w_value, preferred_element_type=jnp.float32)
        .astype(jnp.bfloat16)
        .reshape(rows, value_heads, HD)
    )
    block = min(rows, 512)
    index = jnp.arange(rows, dtype=jnp.int32)

    def one_block(start):
        index_block = start + jnp.arange(block, dtype=jnp.int32)
        scores = jnp.einsum(
            "qkgd,skd->kgqs", query, keyed, preferred_element_type=jnp.float32
        ) * HD ** (-0.5)
        allowed = (segment[:, None] == segment[None, :]) & (index[None, :] <= index_block[:, None])
        scores = jnp.where(allowed[None, None], scores, -1e30)
        highest = jnp.max(scores, axis=-1, keepdims=True)
        expo = jnp.exp(scores - highest)
        weights = (expo / jnp.sum(expo, axis=-1, keepdims=True)).astype(jnp.bfloat16)
        mixed = jnp.einsum("kgqs,skd->qkgd", weights, valued, preferred_element_type=jnp.float32)
        return mixed.astype(jnp.bfloat16).reshape(block, query_heads * HD)

    starts = jnp.arange(rows // block, dtype=jnp.int32) * block
    return lax.map(one_block, starts).reshape(rows, query_heads * HD)


def expert_rows(rows, w_expert_gate, w_expert_up, w_expert_down):
    shape = rows.shape
    flat = rows.reshape(-1, shape[-1])
    gated = jnp.dot(flat, w_expert_gate, preferred_element_type=jnp.float32)
    lifted = jnp.dot(flat, w_expert_up, preferred_element_type=jnp.float32)
    active = (jax.nn.silu(gated) * lifted).astype(jnp.bfloat16)
    return (
        jnp.dot(active, w_expert_down, preferred_element_type=jnp.float32)
        .astype(jnp.bfloat16)
        .reshape(shape)
    )


def per_device(
    tokens,
    segment_ids,
    routes,
    norm_gain,
    w_query,
    w_key,
    w_value,
    w_out,
    ffn_gain,
    w_router,
    w_shared_gate,
    w_shared_up,
    w_shared_down,
    w_expert_gate,
    w_expert_up,
    w_expert_down,
):
    own_rows = tokens[0]
    tok_count = own_rows.shape[0]
    width = own_rows.shape[1]
    normed = rms_norm(own_rows, norm_gain)
    group_rows = gather_ring(normed, "dp")
    group_segments = gather_ring(segment_ids[0], "dp")
    attended = attend(group_rows, group_segments, w_query, w_key, w_value)
    head_sum = scatter_sum(
        jnp.dot(attended, w_out, preferred_element_type=jnp.float32).astype(jnp.bfloat16), "dp"
    )
    residual = (own_rows.astype(jnp.float32) + head_sum).astype(jnp.bfloat16)
    mixed = rms_norm(residual, ffn_gain)
    piece = gather_ring(mixed, "dp")
    gated = jnp.dot(piece, w_shared_gate, preferred_element_type=jnp.float32)
    lifted = jnp.dot(piece, w_shared_up, preferred_element_type=jnp.float32)
    hidden = (jax.nn.silu(gated) * lifted).astype(jnp.bfloat16)
    shared_sum = scatter_sum(
        jnp.dot(hidden, w_shared_down, preferred_element_type=jnp.float32).astype(jnp.bfloat16), "dp"
    )
    expert_count = w_router.shape[1]
    dp_size = lax.axis_size("dp")
    planes = lax.axis_size("zc")
    plane = lax.axis_index("zc")
    capacity = 4 * tok_count * TOP // (3 * expert_count)
    depth = planes * capacity
    slots = dp_size * depth
    mixed_g = lax.all_gather(mixed, "zc", axis=0, tiled=True)
    routes_g = gather_ring(routes[0], "zc")
    rows_g = mixed_g.shape[0]
    labels = jnp.arange(expert_count, dtype=jnp.int32)
    logits = jnp.dot(mixed_g, w_router, preferred_element_type=jnp.float32)
    chosen = jnp.sum(
        jnp.where(routes_g[:, :, None] == labels[None, None, :], logits[:, None, :], 0.0), axis=2
    )
    highest = jnp.max(chosen, axis=1, keepdims=True)
    expo = jnp.exp(chosen - highest)
    gates = expo / jnp.sum(expo, axis=1, keepdims=True)
    route_flat = routes_g.reshape(-1)
    inside = (route_flat % planes) == plane
    dest = route_flat // planes
    onehot = ((dest[:, None] == jnp.arange(dp_size, dtype=jnp.int32)[None, :]) & inside[:, None]).astype(jnp.int32)
    slot = jnp.sum(jnp.cumsum(onehot, axis=0) * onehot, axis=1) - 1
    target = jnp.where(inside, dest * depth + slot, -1).reshape(rows_g, TOP)
    hit = target[:, :, None] == jnp.arange(slots, dtype=jnp.int32)[None, None, :]
    placed = jnp.any(hit, axis=1).astype(jnp.bfloat16)
    send = lax.dot_general(
        placed, mixed_g, (((0,), (0,)), ((), ())), preferred_element_type=jnp.float32
    ).astype(jnp.bfloat16)
    recv = exchange(send.reshape(dp_size, depth, width), "dp")
    mine = recv.reshape(slots, width)
    swap = [(0, 1), (1, 0)]
    other = lax.ppermute(mine, "core", swap)
    half_rows = expert_rows(
        jnp.concatenate([mine, other], axis=0), w_expert_gate, w_expert_up, w_expert_down
    )
    from_partner = lax.ppermute(half_rows[slots:], "core", swap)
    expert_out = (
        half_rows[:slots].astype(jnp.float32) + from_partner.astype(jnp.float32)
    ).astype(jnp.bfloat16)
    back = exchange(expert_out.reshape(dp_size, depth, width), "dp").reshape(slots, width)
    comb = jnp.sum(jnp.where(hit, gates[:, :, None], 0.0), axis=1)
    first = comb.astype(jnp.bfloat16)
    rest = comb - first.astype(jnp.float32)
    second = rest.astype(jnp.bfloat16)
    third = (rest - second.astype(jnp.float32)).astype(jnp.bfloat16)
    partial = (
        jnp.dot(first, back, preferred_element_type=jnp.float32)
        + jnp.dot(second, back, preferred_element_type=jnp.float32)
        + jnp.dot(third, back, preferred_element_type=jnp.float32)
    )
    routed = lax.psum_scatter(
        partial.astype(jnp.bfloat16), "zc", scatter_dimension=0, tiled=True
    ).astype(jnp.float32)
    output = (residual.astype(jnp.float32) + shared_sum + routed).astype(jnp.bfloat16)
    return output[None]


def solution(mesh):
    dp_size = mesh.shape["dp"]
    planes = mesh.shape["expert"] // 2
    fine = jax.sharding.Mesh(mesh.devices.reshape(dp_size, planes, 2), ("dp", "zc", "core"))
    ex = ("zc", "core")
    in_specs = (
        P(ex, "dp", None),
        P(ex, "dp"),
        P(ex, "dp", None),
        P(),
        P(None, "dp"),
        P(None, "dp"),
        P(None, "dp"),
        P("dp", None),
        P(),
        P(),
        P(None, "dp"),
        P(None, "dp"),
        P("dp", None),
        P(None, ("dp",) + ex),
        P(None, ("dp",) + ex),
        P(("dp",) + ex, None),
    )
    out_specs = P(ex, "dp", None)
    return jax.shard_map(
        per_device, mesh=fine, in_specs=in_specs, out_specs=out_specs, check_vma=False
    )
```

```python
import jax
import jax.numpy as jnp
from jax import lax
from jax.sharding import PartitionSpec as P

HD = 128
TOP = 6


epsilon = 1e-06


def shifted(x, axis, n, s):
    return lax.ppermute(x, axis, [(i, (i + s) % n) for i in range(n)])


def ring_gather(x, axis):
    n = lax.axis_size(axis)
    return jnp.stack([x] + [shifted(x, axis, n, s) for s in range(1, n)])


def ring_scatter(blocks, axis):
    n = lax.axis_size(axis)
    total = blocks[0].astype(jnp.float32)
    for s in range(1, n):
        total = total + shifted(blocks[s], axis, n, n - s).astype(jnp.float32)
    return total


def ring_out(x, axis):
    n = lax.axis_size(axis)
    return jnp.stack([x[0]] + [shifted(x[s], axis, n, s) for s in range(1, n)])


def ring_back(x, axis):
    n = lax.axis_size(axis)
    return jnp.stack([x[0]] + [shifted(x[s], axis, n, n - s) for s in range(1, n)])

def rms_norm(values, gain):
    wide = values.astype(jnp.float32)
    scale = lax.rsqrt(jnp.mean(wide * wide, axis=-1, keepdims=True) + epsilon)
    return (wide * scale * gain).astype(jnp.bfloat16)


def positions(segment, index):
    same = (segment[:, None] == segment[None, :]) & (index[None, :] < index[:, None])
    return jnp.sum(same.astype(jnp.int32), axis=1)


def rotate(heads, place):
    half = heads.shape[-1] // 2
    freq = 10000.0 ** (-jnp.arange(half, dtype=jnp.float32) / half)
    angle = place.astype(jnp.float32)[:, None] * freq[None, :]
    cosine = jnp.cos(angle)[:, None, :]
    sine = jnp.sin(angle)[:, None, :]
    first = heads[..., :half]
    second = heads[..., half:]
    return jnp.concatenate(
        [first * cosine - second * sine, second * cosine + first * sine], axis=-1
    )


def attend(normed, segment, index, w_query, w_key, w_value):
    rows = normed.shape[0]
    query_heads = w_query.shape[1] // HD
    value_heads = w_key.shape[1] // HD
    group_size = query_heads // value_heads
    place = positions(segment, index)
    query = jnp.dot(normed, w_query, preferred_element_type=jnp.float32).reshape(
        rows, query_heads, HD
    )
    query = rotate(query, place).astype(jnp.bfloat16).reshape(rows, value_heads, group_size, HD)
    keyed = jnp.dot(normed, w_key, preferred_element_type=jnp.float32).reshape(
        rows, value_heads, HD
    )
    keyed = rotate(keyed, place).astype(jnp.bfloat16)
    valued = (
        jnp.dot(normed, w_value, preferred_element_type=jnp.float32)
        .astype(jnp.bfloat16)
        .reshape(rows, value_heads, HD)
    )
    block = min(rows, 512)

    def one_block(start):
        index_block = lax.dynamic_slice_in_dim(index, start, block, 0)
        scores = jnp.einsum(
            "qkgd,skd->kgqs", query, keyed, preferred_element_type=jnp.float32
        ) * HD ** (-0.5)
        allowed = (segment[:, None] == segment[None, :]) & (index[None, :] <= index_block[:, None])
        scores = jnp.where(allowed[None, None], scores, -1e30)
        highest = jnp.max(scores, axis=-1, keepdims=True)
        expo = jnp.exp(scores - highest)
        weights = (expo / jnp.sum(expo, axis=-1, keepdims=True)).astype(jnp.bfloat16)
        mixed = jnp.einsum("kgqs,skd->qkgd", weights, valued, preferred_element_type=jnp.float32)
        return mixed.astype(jnp.bfloat16).reshape(block, query_heads * HD)

    starts = jnp.arange(rows // block, dtype=jnp.int32) * block
    return lax.map(one_block, starts).reshape(rows, query_heads * HD)


def expert_rows(rows, w_expert_gate, w_expert_up, w_expert_down):
    shape = rows.shape
    flat = rows.reshape(-1, shape[-1])
    gated = jnp.dot(flat, w_expert_gate, preferred_element_type=jnp.float32)
    lifted = jnp.dot(flat, w_expert_up, preferred_element_type=jnp.float32)
    active = (jax.nn.silu(gated) * lifted).astype(jnp.bfloat16)
    return (
        jnp.dot(active, w_expert_down, preferred_element_type=jnp.float32)
        .astype(jnp.bfloat16)
        .reshape(shape)
    )


def per_device(
    tokens,
    segment_ids,
    routes,
    norm_gain,
    w_query,
    w_key,
    w_value,
    w_out,
    ffn_gain,
    w_router,
    w_shared_gate,
    w_shared_up,
    w_shared_down,
    w_expert_gate,
    w_expert_up,
    w_expert_down,
):
    own_rows = tokens[0]
    tok_count = own_rows.shape[0]
    width = own_rows.shape[1]
    normed = rms_norm(own_rows, norm_gain)
    dp_size = lax.axis_size("dp")
    me_dp = lax.axis_index("dp")
    group_rows = ring_gather(normed, "dp").reshape(dp_size * tok_count, width)
    group_segments = ring_gather(segment_ids[0], "dp").reshape(-1)
    home = (me_dp - jnp.arange(dp_size, dtype=jnp.int32)) % dp_size
    group_index = (home[:, None] * tok_count + jnp.arange(tok_count, dtype=jnp.int32)[None, :]).reshape(-1)
    attended = attend(group_rows, group_segments, group_index, w_query, w_key, w_value)
    head_sum = ring_scatter(
        jnp.dot(attended, w_out, preferred_element_type=jnp.float32)
        .astype(jnp.bfloat16)
        .reshape(dp_size, tok_count, width),
        "dp",
    )
    residual = (own_rows.astype(jnp.float32) + head_sum).astype(jnp.bfloat16)
    mixed = rms_norm(residual, ffn_gain)
    piece = ring_gather(mixed, "dp").reshape(dp_size * tok_count, width)
    gated = jnp.dot(piece, w_shared_gate, preferred_element_type=jnp.float32)
    lifted = jnp.dot(piece, w_shared_up, preferred_element_type=jnp.float32)
    hidden = (jax.nn.silu(gated) * lifted).astype(jnp.bfloat16)
    shared_part = (
        jnp.dot(hidden, w_shared_down, preferred_element_type=jnp.float32)
        .astype(jnp.bfloat16)
        .reshape(dp_size, tok_count, width)
    )
    expert_count = w_router.shape[1]
    planes = lax.axis_size("zc")
    plane = lax.axis_index("zc")
    capacity = 4 * tok_count * TOP // (3 * expert_count)
    depth = planes * capacity
    slots = dp_size * depth
    mixed_g = lax.all_gather(mixed, "zc", axis=0, tiled=True)
    mixed_g, shared_part = lax.optimization_barrier((mixed_g, shared_part))
    routes_rel = ring_gather(routes[0], "zc")
    routes_g = jnp.take(routes_rel, (plane - jnp.arange(planes, dtype=jnp.int32)) % planes, axis=0)
    routes_g = routes_g.reshape(planes * tok_count, TOP)
    rows_g = mixed_g.shape[0]
    labels = jnp.arange(expert_count, dtype=jnp.int32)
    logits = jnp.dot(mixed_g, w_router, preferred_element_type=jnp.float32)
    chosen = jnp.sum(
        jnp.where(routes_g[:, :, None] == labels[None, None, :], logits[:, None, :], 0.0), axis=2
    )
    highest = jnp.max(chosen, axis=1, keepdims=True)
    expo = jnp.exp(chosen - highest)
    gates = expo / jnp.sum(expo, axis=1, keepdims=True)
    route_flat = routes_g.reshape(-1)
    inside = (route_flat % planes) == plane
    dest = (route_flat // planes - me_dp) % dp_size
    onehot = ((dest[:, None] == jnp.arange(dp_size, dtype=jnp.int32)[None, :]) & inside[:, None]).astype(jnp.int32)
    slot = jnp.sum(jnp.cumsum(onehot, axis=0) * onehot, axis=1) - 1
    target = jnp.where(inside, dest * depth + slot, -1).reshape(rows_g, TOP)
    hit = target[:, :, None] == jnp.arange(slots, dtype=jnp.int32)[None, None, :]
    placed = jnp.any(hit, axis=1).astype(jnp.bfloat16)
    send = lax.dot_general(
        placed, mixed_g, (((0,), (0,)), ((), ())), preferred_element_type=jnp.float32
    ).astype(jnp.bfloat16)
    recv = ring_out(send.reshape(dp_size, depth, width), "dp")
    mine = recv.reshape(slots, width)
    swap = [(0, 1), (1, 0)]
    other = lax.ppermute(mine, "core", swap)
    half_rows = expert_rows(
        jnp.concatenate([mine, other], axis=0), w_expert_gate, w_expert_up, w_expert_down
    )
    from_partner = lax.ppermute(half_rows[slots:], "core", swap)
    expert_out = (
        half_rows[:slots].astype(jnp.float32) + from_partner.astype(jnp.float32)
    ).astype(jnp.bfloat16)
    back = ring_back(expert_out.reshape(dp_size, depth, width), "dp").reshape(slots, width)
    comb = jnp.sum(jnp.where(hit, gates[:, :, None], 0.0), axis=1)
    first = comb.astype(jnp.bfloat16)
    rest = comb - first.astype(jnp.float32)
    second = rest.astype(jnp.bfloat16)
    third = (rest - second.astype(jnp.float32)).astype(jnp.bfloat16)
    partial = (
        jnp.dot(first, back, preferred_element_type=jnp.float32)
        + jnp.dot(second, back, preferred_element_type=jnp.float32)
        + jnp.dot(third, back, preferred_element_type=jnp.float32)
    )
    routed = lax.psum_scatter(
        partial.astype(jnp.bfloat16), "zc", scatter_dimension=0, tiled=True
    ).astype(jnp.float32)
    shared_sum = ring_scatter(shared_part, "dp")
    output = (residual.astype(jnp.float32) + shared_sum + routed).astype(jnp.bfloat16)
    return output[None]


def solution(mesh):
    dp_size = mesh.shape["dp"]
    planes = mesh.shape["expert"] // 2
    fine = jax.sharding.Mesh(mesh.devices.reshape(dp_size, planes, 2), ("dp", "zc", "core"))
    ex = ("zc", "core")
    in_specs = (
        P(ex, "dp", None),
        P(ex, "dp"),
        P(ex, "dp", None),
        P(),
        P(None, "dp"),
        P(None, "dp"),
        P(None, "dp"),
        P("dp", None),
        P(),
        P(),
        P(None, "dp"),
        P(None, "dp"),
        P("dp", None),
        P(None, ("dp",) + ex),
        P(None, ("dp",) + ex),
        P(("dp",) + ex, None),
    )
    out_specs = P(ex, "dp", None)
    return jax.shard_map(
        per_device, mesh=fine, in_specs=in_specs, out_specs=out_specs, check_vma=False
    )
```

```python
import jax
import jax.numpy as jnp
from jax import lax
from jax.sharding import PartitionSpec as P

HD = 128
TOP = 6


epsilon = 1e-06


def shifted(x, axis, n, s):
    return lax.ppermute(x, axis, [(i, (i + s) % n) for i in range(n)])


def ring_gather(x, axis):
    n = lax.axis_size(axis)
    return jnp.stack([x] + [shifted(x, axis, n, s) for s in range(1, n)])


def ring_scatter(blocks, axis):
    n = lax.axis_size(axis)
    total = blocks[0].astype(jnp.float32)
    for s in range(1, n):
        total = total + shifted(blocks[s], axis, n, n - s).astype(jnp.float32)
    return total


def ring_out(x, axis):
    n = lax.axis_size(axis)
    return jnp.stack([x[0]] + [shifted(x[s], axis, n, s) for s in range(1, n)])


def ring_back(x, axis):
    n = lax.axis_size(axis)
    return jnp.stack([x[0]] + [shifted(x[s], axis, n, n - s) for s in range(1, n)])

def rms_norm(values, gain):
    wide = values.astype(jnp.float32)
    scale = lax.rsqrt(jnp.mean(wide * wide, axis=-1, keepdims=True) + epsilon)
    return (wide * scale * gain).astype(jnp.bfloat16)


def positions(segment, index):
    same = (segment[:, None] == segment[None, :]) & (index[None, :] < index[:, None])
    return jnp.sum(same.astype(jnp.int32), axis=1)


def rotate(heads, place):
    half = heads.shape[-1] // 2
    freq = 10000.0 ** (-jnp.arange(half, dtype=jnp.float32) / half)
    angle = place.astype(jnp.float32)[:, None] * freq[None, :]
    cosine = jnp.cos(angle)[:, None, :]
    sine = jnp.sin(angle)[:, None, :]
    first = heads[..., :half]
    second = heads[..., half:]
    return jnp.concatenate(
        [first * cosine - second * sine, second * cosine + first * sine], axis=-1
    )


def attend(normed, segment, index, w_query, w_key, w_value):
    rows = normed.shape[0]
    query_heads = w_query.shape[1] // HD
    value_heads = w_key.shape[1] // HD
    group_size = query_heads // value_heads
    place = positions(segment, index)
    query = jnp.dot(normed, w_query, preferred_element_type=jnp.float32).reshape(
        rows, query_heads, HD
    )
    query = rotate(query, place).astype(jnp.bfloat16).reshape(rows, value_heads, group_size, HD)
    keyed = jnp.dot(normed, w_key, preferred_element_type=jnp.float32).reshape(
        rows, value_heads, HD
    )
    keyed = rotate(keyed, place).astype(jnp.bfloat16)
    valued = (
        jnp.dot(normed, w_value, preferred_element_type=jnp.float32)
        .astype(jnp.bfloat16)
        .reshape(rows, value_heads, HD)
    )
    block = min(rows, 512)

    def one_block(start):
        index_block = lax.dynamic_slice_in_dim(index, start, block, 0)
        scores = jnp.einsum(
            "qkgd,skd->kgqs", query, keyed, preferred_element_type=jnp.float32
        ) * HD ** (-0.5)
        allowed = (segment[:, None] == segment[None, :]) & (index[None, :] <= index_block[:, None])
        scores = jnp.where(allowed[None, None], scores, -1e30)
        highest = jnp.max(scores, axis=-1, keepdims=True)
        expo = jnp.exp(scores - highest)
        weights = (expo / jnp.sum(expo, axis=-1, keepdims=True)).astype(jnp.bfloat16)
        mixed = jnp.einsum("kgqs,skd->qkgd", weights, valued, preferred_element_type=jnp.float32)
        return mixed.astype(jnp.bfloat16).reshape(block, query_heads * HD)

    starts = jnp.arange(rows // block, dtype=jnp.int32) * block
    return lax.map(one_block, starts).reshape(rows, query_heads * HD)


def expert_rows(rows, w_expert_gate, w_expert_up, w_expert_down):
    shape = rows.shape
    flat = rows.reshape(-1, shape[-1])
    gated = jnp.dot(flat, w_expert_gate, preferred_element_type=jnp.float32)
    lifted = jnp.dot(flat, w_expert_up, preferred_element_type=jnp.float32)
    active = (jax.nn.silu(gated) * lifted).astype(jnp.bfloat16)
    return (
        jnp.dot(active, w_expert_down, preferred_element_type=jnp.float32)
        .astype(jnp.bfloat16)
        .reshape(shape)
    )


def per_device(
    tokens,
    segment_ids,
    routes,
    norm_gain,
    w_query,
    w_key,
    w_value,
    w_out,
    ffn_gain,
    w_router,
    w_shared_gate,
    w_shared_up,
    w_shared_down,
    w_expert_gate,
    w_expert_up,
    w_expert_down,
):
    own_rows = tokens[0]
    tok_count = own_rows.shape[0]
    width = own_rows.shape[1]
    normed = rms_norm(own_rows, norm_gain)
    dp_size = lax.axis_size("dp")
    me_dp = lax.axis_index("dp")
    group_rows = ring_gather(normed, "dp").reshape(dp_size * tok_count, width)
    group_segments = ring_gather(segment_ids[0], "dp").reshape(-1)
    home = (me_dp - jnp.arange(dp_size, dtype=jnp.int32)) % dp_size
    group_index = (home[:, None] * tok_count + jnp.arange(tok_count, dtype=jnp.int32)[None, :]).reshape(-1)
    attended = attend(group_rows, group_segments, group_index, w_query, w_key, w_value)
    head_sum = ring_scatter(
        jnp.dot(attended, w_out, preferred_element_type=jnp.float32)
        .astype(jnp.bfloat16)
        .reshape(dp_size, tok_count, width),
        "dp",
    )
    residual = (own_rows.astype(jnp.float32) + head_sum).astype(jnp.bfloat16)
    mixed = rms_norm(residual, ffn_gain)
    piece = ring_gather(mixed, "dp").reshape(dp_size * tok_count, width)
    gated = jnp.dot(piece, w_shared_gate, preferred_element_type=jnp.float32)
    lifted = jnp.dot(piece, w_shared_up, preferred_element_type=jnp.float32)
    hidden = (jax.nn.silu(gated) * lifted).astype(jnp.bfloat16)
    shared_part = (
        jnp.dot(hidden, w_shared_down, preferred_element_type=jnp.float32)
        .astype(jnp.bfloat16)
        .reshape(dp_size, tok_count, width)
    )
    expert_count = w_router.shape[1]
    planes = lax.axis_size("zc")
    plane = lax.axis_index("zc")
    capacity = 4 * tok_count * TOP // (3 * expert_count)
    depth = planes * capacity
    slots = dp_size * depth
    mixed_g = lax.all_gather(mixed, "zc", axis=0, tiled=True)
    mixed_g, shared_part = lax.optimization_barrier((mixed_g, shared_part))
    routes_rel = ring_gather(routes[0], "zc")
    routes_g = jnp.take(routes_rel, (plane - jnp.arange(planes, dtype=jnp.int32)) % planes, axis=0)
    routes_g = routes_g.reshape(planes * tok_count, TOP)
    rows_g = mixed_g.shape[0]
    labels = jnp.arange(expert_count, dtype=jnp.int32)
    logits = jnp.dot(mixed_g, w_router, preferred_element_type=jnp.float32)
    chosen = jnp.sum(
        jnp.where(routes_g[:, :, None] == labels[None, None, :], logits[:, None, :], 0.0), axis=2
    )
    highest = jnp.max(chosen, axis=1, keepdims=True)
    expo = jnp.exp(chosen - highest)
    gates = expo / jnp.sum(expo, axis=1, keepdims=True)
    route_flat = routes_g.reshape(-1)
    inside = (route_flat % planes) == plane
    dest = (route_flat // planes - me_dp) % dp_size
    onehot = ((dest[:, None] == jnp.arange(dp_size, dtype=jnp.int32)[None, :]) & inside[:, None]).astype(jnp.int32)
    slot = jnp.sum(jnp.cumsum(onehot, axis=0) * onehot, axis=1) - 1
    target = jnp.where(inside, dest * depth + slot, -1).reshape(rows_g, TOP)
    hit = target[:, :, None] == jnp.arange(slots, dtype=jnp.int32)[None, None, :]
    placed = jnp.any(hit, axis=1).astype(jnp.bfloat16)
    send = lax.dot_general(
        placed, mixed_g, (((0,), (0,)), ((), ())), preferred_element_type=jnp.float32
    ).astype(jnp.bfloat16)
    recv = ring_out(send.reshape(dp_size, depth, width), "dp")
    recv, shared_part = lax.optimization_barrier((recv, shared_part))
    shared_sum = ring_scatter(shared_part, "dp")
    mine = recv.reshape(slots, width)
    swap = [(0, 1), (1, 0)]
    other = lax.ppermute(mine, "core", swap)
    both = jnp.concatenate([mine, other], axis=0)
    gated_e = jnp.dot(both, w_expert_gate, preferred_element_type=jnp.float32)
    lifted_e = jnp.dot(both, w_expert_up, preferred_element_type=jnp.float32)
    active = (jax.nn.silu(gated_e) * lifted_e).astype(jnp.bfloat16)
    comb = jnp.sum(jnp.where(hit, gates[:, :, None], 0.0), axis=1)
    first = comb.astype(jnp.bfloat16)
    rest = comb - first.astype(jnp.float32)
    second = rest.astype(jnp.bfloat16)
    third = (rest - second.astype(jnp.float32)).astype(jnp.bfloat16)
    halves = 2
    span = width // halves
    routed_parts = []
    for h in range(halves):
        cols = slice(h * span, (h + 1) * span)
        half_rows = jnp.dot(
            active, w_expert_down[:, cols], preferred_element_type=jnp.float32
        ).astype(jnp.bfloat16)
        from_partner = lax.ppermute(half_rows[slots:], "core", swap)
        expert_out = (
            half_rows[:slots].astype(jnp.float32) + from_partner.astype(jnp.float32)
        ).astype(jnp.bfloat16)
        if h == 0:
            expert_out, shared_sum = lax.optimization_barrier((expert_out, shared_sum))
        back = ring_back(expert_out.reshape(dp_size, depth, span), "dp").reshape(slots, span)
        partial = (
            jnp.dot(first, back, preferred_element_type=jnp.float32)
            + jnp.dot(second, back, preferred_element_type=jnp.float32)
            + jnp.dot(third, back, preferred_element_type=jnp.float32)
        )
        routed_parts.append(
            lax.psum_scatter(partial.astype(jnp.bfloat16), "zc", scatter_dimension=0, tiled=True)
        )
    routed = jnp.concatenate(routed_parts, axis=1).astype(jnp.float32)
    output = (residual.astype(jnp.float32) + shared_sum + routed).astype(jnp.bfloat16)
    return output[None]


def solution(mesh):
    dp_size = mesh.shape["dp"]
    planes = mesh.shape["expert"] // 2
    fine = jax.sharding.Mesh(mesh.devices.reshape(dp_size, planes, 2), ("dp", "zc", "core"))
    ex = ("zc", "core")
    in_specs = (
        P(ex, "dp", None),
        P(ex, "dp"),
        P(ex, "dp", None),
        P(),
        P(None, "dp"),
        P(None, "dp"),
        P(None, "dp"),
        P("dp", None),
        P(),
        P(),
        P(None, "dp"),
        P(None, "dp"),
        P("dp", None),
        P(None, ("dp",) + ex),
        P(None, ("dp",) + ex),
        P(("dp",) + ex, None),
    )
    out_specs = P(ex, "dp", None)
    return jax.shard_map(
        per_device, mesh=fine, in_specs=in_specs, out_specs=out_specs, check_vma=False
    )
```

```python
import jax
import jax.numpy as jnp
from jax import lax
from jax.sharding import PartitionSpec as P

HD = 128
TOP = 6


epsilon = 1e-06


def shifted(x, axis, n, s):
    return lax.ppermute(x, axis, [(i, (i + s) % n) for i in range(n)])


def ring_gather(x, axis):
    n = lax.axis_size(axis)
    return jnp.stack([x] + [shifted(x, axis, n, s) for s in range(1, n)])


def ring_scatter(blocks, axis):
    n = lax.axis_size(axis)
    total = blocks[0].astype(jnp.float32)
    for s in range(1, n):
        total = total + shifted(blocks[s], axis, n, n - s).astype(jnp.float32)
    return total


def ring_out(x, axis):
    n = lax.axis_size(axis)
    return jnp.stack([x[0]] + [shifted(x[s], axis, n, s) for s in range(1, n)])


def ring_back(x, axis):
    n = lax.axis_size(axis)
    return jnp.stack([x[0]] + [shifted(x[s], axis, n, n - s) for s in range(1, n)])

def rms_norm(values, gain):
    wide = values.astype(jnp.float32)
    scale = lax.rsqrt(jnp.mean(wide * wide, axis=-1, keepdims=True) + epsilon)
    return (wide * scale * gain).astype(jnp.bfloat16)


def positions(segment, index):
    same = (segment[:, None] == segment[None, :]) & (index[None, :] < index[:, None])
    return jnp.sum(same.astype(jnp.int32), axis=1)


def rotate(heads, place):
    half = heads.shape[-1] // 2
    freq = 10000.0 ** (-jnp.arange(half, dtype=jnp.float32) / half)
    angle = place.astype(jnp.float32)[:, None] * freq[None, :]
    cosine = jnp.cos(angle)[:, None, :]
    sine = jnp.sin(angle)[:, None, :]
    first = heads[..., :half]
    second = heads[..., half:]
    return jnp.concatenate(
        [first * cosine - second * sine, second * cosine + first * sine], axis=-1
    )


def attend(normed, segment, index, w_query, w_key, w_value):
    rows = normed.shape[0]
    query_heads = w_query.shape[1] // HD
    value_heads = w_key.shape[1] // HD
    group_size = query_heads // value_heads
    place = positions(segment, index)
    query = jnp.dot(normed, w_query, preferred_element_type=jnp.float32).reshape(
        rows, query_heads, HD
    )
    query = rotate(query, place).astype(jnp.bfloat16).reshape(rows, value_heads, group_size, HD)
    keyed = jnp.dot(normed, w_key, preferred_element_type=jnp.float32).reshape(
        rows, value_heads, HD
    )
    keyed = rotate(keyed, place).astype(jnp.bfloat16)
    valued = (
        jnp.dot(normed, w_value, preferred_element_type=jnp.float32)
        .astype(jnp.bfloat16)
        .reshape(rows, value_heads, HD)
    )
    block = min(rows, 512)

    def one_block(start):
        index_block = lax.dynamic_slice_in_dim(index, start, block, 0)
        scores = jnp.einsum(
            "qkgd,skd->kgqs", query, keyed, preferred_element_type=jnp.float32
        ) * HD ** (-0.5)
        allowed = (segment[:, None] == segment[None, :]) & (index[None, :] <= index_block[:, None])
        scores = jnp.where(allowed[None, None], scores, -1e30)
        highest = jnp.max(scores, axis=-1, keepdims=True)
        expo = jnp.exp(scores - highest)
        weights = (expo / jnp.sum(expo, axis=-1, keepdims=True)).astype(jnp.bfloat16)
        mixed = jnp.einsum("kgqs,skd->qkgd", weights, valued, preferred_element_type=jnp.float32)
        return mixed.astype(jnp.bfloat16).reshape(block, query_heads * HD)

    starts = jnp.arange(rows // block, dtype=jnp.int32) * block
    return lax.map(one_block, starts).reshape(rows, query_heads * HD)


def expert_rows(rows, w_expert_gate, w_expert_up, w_expert_down):
    shape = rows.shape
    flat = rows.reshape(-1, shape[-1])
    gated = jnp.dot(flat, w_expert_gate, preferred_element_type=jnp.float32)
    lifted = jnp.dot(flat, w_expert_up, preferred_element_type=jnp.float32)
    active = (jax.nn.silu(gated) * lifted).astype(jnp.bfloat16)
    return (
        jnp.dot(active, w_expert_down, preferred_element_type=jnp.float32)
        .astype(jnp.bfloat16)
        .reshape(shape)
    )


def per_device(
    tokens,
    segment_ids,
    routes,
    norm_gain,
    w_query,
    w_key,
    w_value,
    w_out,
    ffn_gain,
    w_router,
    w_shared_gate,
    w_shared_up,
    w_shared_down,
    w_expert_gate,
    w_expert_up,
    w_expert_down,
):
    own_rows = tokens[0]
    tok_count = own_rows.shape[0]
    width = own_rows.shape[1]
    normed = rms_norm(own_rows, norm_gain)
    dp_size = lax.axis_size("dp")
    me_dp = lax.axis_index("dp")
    group_rows = ring_gather(normed, "dp").reshape(dp_size * tok_count, width)
    group_segments = ring_gather(segment_ids[0], "dp").reshape(-1)
    home = (me_dp - jnp.arange(dp_size, dtype=jnp.int32)) % dp_size
    group_index = (home[:, None] * tok_count + jnp.arange(tok_count, dtype=jnp.int32)[None, :]).reshape(-1)
    attended = attend(group_rows, group_segments, group_index, w_query, w_key, w_value)
    head_sum = ring_scatter(
        jnp.dot(attended, w_out, preferred_element_type=jnp.float32)
        .astype(jnp.bfloat16)
        .reshape(dp_size, tok_count, width),
        "dp",
    )
    residual = (own_rows.astype(jnp.float32) + head_sum).astype(jnp.bfloat16)
    mixed = rms_norm(residual, ffn_gain)
    piece = ring_gather(mixed, "dp").reshape(dp_size * tok_count, width)
    gated = jnp.dot(piece, w_shared_gate, preferred_element_type=jnp.float32)
    lifted = jnp.dot(piece, w_shared_up, preferred_element_type=jnp.float32)
    hidden = (jax.nn.silu(gated) * lifted).astype(jnp.bfloat16)
    shared_part = (
        jnp.dot(hidden, w_shared_down, preferred_element_type=jnp.float32)
        .astype(jnp.bfloat16)
        .reshape(dp_size, tok_count, width)
    )
    expert_count = w_router.shape[1]
    planes = lax.axis_size("zc")
    plane = lax.axis_index("zc")
    capacity = 4 * tok_count * TOP // (3 * expert_count)
    depth = planes * capacity
    slots = dp_size * depth
    mixed_g = ring_gather(mixed, "zc").reshape(planes * tok_count, width)
    mixed_g, shared_part = lax.optimization_barrier((mixed_g, shared_part))
    routes_g = ring_gather(routes[0], "zc").reshape(planes * tok_count, TOP)
    rows_g = mixed_g.shape[0]
    labels = jnp.arange(expert_count, dtype=jnp.int32)
    logits = jnp.dot(mixed_g, w_router, preferred_element_type=jnp.float32)
    chosen = jnp.sum(
        jnp.where(routes_g[:, :, None] == labels[None, None, :], logits[:, None, :], 0.0), axis=2
    )
    highest = jnp.max(chosen, axis=1, keepdims=True)
    expo = jnp.exp(chosen - highest)
    gates = expo / jnp.sum(expo, axis=1, keepdims=True)
    route_flat = routes_g.reshape(-1)
    inside = (route_flat % planes) == plane
    dest = (route_flat // planes - me_dp) % dp_size
    onehot = ((dest[:, None] == jnp.arange(dp_size, dtype=jnp.int32)[None, :]) & inside[:, None]).astype(jnp.int32)
    slot = jnp.sum(jnp.cumsum(onehot, axis=0) * onehot, axis=1) - 1
    target = jnp.where(inside, dest * depth + slot, -1).reshape(rows_g, TOP)
    hit = target[:, :, None] == jnp.arange(slots, dtype=jnp.int32)[None, None, :]
    placed = jnp.any(hit, axis=1).astype(jnp.bfloat16)
    send = lax.dot_general(
        placed, mixed_g, (((0,), (0,)), ((), ())), preferred_element_type=jnp.float32
    ).astype(jnp.bfloat16)
    recv = ring_out(send.reshape(dp_size, depth, width), "dp")
    mine = recv.reshape(slots, width)
    swap = [(0, 1), (1, 0)]
    other = lax.ppermute(mine, "core", swap)
    half_rows = expert_rows(
        jnp.concatenate([mine, other], axis=0), w_expert_gate, w_expert_up, w_expert_down
    )
    from_partner = lax.ppermute(half_rows[slots:], "core", swap)
    expert_out = (
        half_rows[:slots].astype(jnp.float32) + from_partner.astype(jnp.float32)
    ).astype(jnp.bfloat16)
    back = ring_back(expert_out.reshape(dp_size, depth, width), "dp").reshape(slots, width)
    comb = jnp.sum(jnp.where(hit, gates[:, :, None], 0.0), axis=1)
    first = comb.astype(jnp.bfloat16)
    rest = comb - first.astype(jnp.float32)
    second = rest.astype(jnp.bfloat16)
    third = (rest - second.astype(jnp.float32)).astype(jnp.bfloat16)
    partial = (
        jnp.dot(first, back, preferred_element_type=jnp.float32)
        + jnp.dot(second, back, preferred_element_type=jnp.float32)
        + jnp.dot(third, back, preferred_element_type=jnp.float32)
    )
    routed = ring_scatter(partial.astype(jnp.bfloat16).reshape(planes, tok_count, width), "zc")
    shared_sum = ring_scatter(shared_part, "dp")
    output = (residual.astype(jnp.float32) + shared_sum + routed).astype(jnp.bfloat16)
    return output[None]


def solution(mesh):
    dp_size = mesh.shape["dp"]
    planes = mesh.shape["expert"] // 2
    fine = jax.sharding.Mesh(mesh.devices.reshape(dp_size, planes, 2), ("dp", "zc", "core"))
    ex = ("zc", "core")
    in_specs = (
        P(ex, "dp", None),
        P(ex, "dp"),
        P(ex, "dp", None),
        P(),
        P(None, "dp"),
        P(None, "dp"),
        P(None, "dp"),
        P("dp", None),
        P(),
        P(),
        P(None, "dp"),
        P(None, "dp"),
        P("dp", None),
        P(None, ("dp",) + ex),
        P(None, ("dp",) + ex),
        P(("dp",) + ex, None),
    )
    out_specs = P(ex, "dp", None)
    return jax.shard_map(
        per_device, mesh=fine, in_specs=in_specs, out_specs=out_specs, check_vma=False
    )
```

```python
import jax
import jax.numpy as jnp
from jax import lax
from jax.sharding import PartitionSpec as P

HD = 128
TOP = 6


epsilon = 1e-06


def shifted(x, axis, n, s):
    return lax.ppermute(x, axis, [(i, (i + s) % n) for i in range(n)])


def ring_gather(x, axis):
    n = lax.axis_size(axis)
    return jnp.stack([x] + [shifted(x, axis, n, s) for s in range(1, n)])


def ring_scatter(blocks, axis):
    n = lax.axis_size(axis)
    total = blocks[0].astype(jnp.float32)
    for s in range(1, n):
        total = total + shifted(blocks[s], axis, n, n - s).astype(jnp.float32)
    return total


def ring_out(x, axis):
    n = lax.axis_size(axis)
    return jnp.stack([x[0]] + [shifted(x[s], axis, n, s) for s in range(1, n)])


def ring_back(x, axis):
    n = lax.axis_size(axis)
    return jnp.stack([x[0]] + [shifted(x[s], axis, n, n - s) for s in range(1, n)])

def rms_norm(values, gain):
    wide = values.astype(jnp.float32)
    scale = lax.rsqrt(jnp.mean(wide * wide, axis=-1, keepdims=True) + epsilon)
    return (wide * scale * gain).astype(jnp.bfloat16)


def positions(segment, index):
    same = (segment[:, None] == segment[None, :]) & (index[None, :] < index[:, None])
    return jnp.sum(same.astype(jnp.int32), axis=1)


def rotate(heads, place):
    half = heads.shape[-1] // 2
    freq = 10000.0 ** (-jnp.arange(half, dtype=jnp.float32) / half)
    angle = place.astype(jnp.float32)[:, None] * freq[None, :]
    cosine = jnp.cos(angle)[:, None, :]
    sine = jnp.sin(angle)[:, None, :]
    first = heads[..., :half]
    second = heads[..., half:]
    return jnp.concatenate(
        [first * cosine - second * sine, second * cosine + first * sine], axis=-1
    )


def attend(normed, segment, index, w_query, w_key, w_value):
    rows = normed.shape[0]
    query_heads = w_query.shape[1] // HD
    value_heads = w_key.shape[1] // HD
    group_size = query_heads // value_heads
    place = positions(segment, index)
    query = jnp.dot(normed, w_query, preferred_element_type=jnp.float32).reshape(
        rows, query_heads, HD
    )
    query = rotate(query, place).astype(jnp.bfloat16).reshape(rows, value_heads, group_size, HD)
    keyed = jnp.dot(normed, w_key, preferred_element_type=jnp.float32).reshape(
        rows, value_heads, HD
    )
    keyed = rotate(keyed, place).astype(jnp.bfloat16)
    valued = (
        jnp.dot(normed, w_value, preferred_element_type=jnp.float32)
        .astype(jnp.bfloat16)
        .reshape(rows, value_heads, HD)
    )
    block = min(rows, 512)

    def one_block(start):
        index_block = lax.dynamic_slice_in_dim(index, start, block, 0)
        scores = jnp.einsum(
            "qkgd,skd->kgqs", query, keyed, preferred_element_type=jnp.float32
        ) * HD ** (-0.5)
        allowed = (segment[:, None] == segment[None, :]) & (index[None, :] <= index_block[:, None])
        scores = jnp.where(allowed[None, None], scores, -1e30)
        highest = jnp.max(scores, axis=-1, keepdims=True)
        expo = jnp.exp(scores - highest)
        weights = (expo / jnp.sum(expo, axis=-1, keepdims=True)).astype(jnp.bfloat16)
        mixed = jnp.einsum("kgqs,skd->qkgd", weights, valued, preferred_element_type=jnp.float32)
        return mixed.astype(jnp.bfloat16).reshape(block, query_heads * HD)

    starts = jnp.arange(rows // block, dtype=jnp.int32) * block
    return lax.map(one_block, starts).reshape(rows, query_heads * HD)


def expert_rows(rows, w_expert_gate, w_expert_up, w_expert_down):
    shape = rows.shape
    flat = rows.reshape(-1, shape[-1])
    gated = jnp.dot(flat, w_expert_gate, preferred_element_type=jnp.float32)
    lifted = jnp.dot(flat, w_expert_up, preferred_element_type=jnp.float32)
    active = (jax.nn.silu(gated) * lifted).astype(jnp.bfloat16)
    return (
        jnp.dot(active, w_expert_down, preferred_element_type=jnp.float32)
        .astype(jnp.bfloat16)
        .reshape(shape)
    )


def per_device(
    tokens,
    segment_ids,
    routes,
    norm_gain,
    w_query,
    w_key,
    w_value,
    w_out,
    ffn_gain,
    w_router,
    w_shared_gate,
    w_shared_up,
    w_shared_down,
    w_expert_gate,
    w_expert_up,
    w_expert_down,
):
    own_rows = tokens[0]
    tok_count = own_rows.shape[0]
    width = own_rows.shape[1]
    normed = rms_norm(own_rows, norm_gain)
    dp_size = lax.axis_size("dp")
    me_dp = lax.axis_index("dp")
    group_rows = ring_gather(normed, "dp").reshape(dp_size * tok_count, width)
    group_segments = ring_gather(segment_ids[0], "dp").reshape(-1)
    home = (me_dp - jnp.arange(dp_size, dtype=jnp.int32)) % dp_size
    group_index = (home[:, None] * tok_count + jnp.arange(tok_count, dtype=jnp.int32)[None, :]).reshape(-1)
    attended = attend(group_rows, group_segments, group_index, w_query, w_key, w_value)
    head_sum = ring_scatter(
        jnp.dot(attended, w_out, preferred_element_type=jnp.float32)
        .astype(jnp.bfloat16)
        .reshape(dp_size, tok_count, width),
        "dp",
    )
    residual = (own_rows.astype(jnp.float32) + head_sum).astype(jnp.bfloat16)
    mixed = rms_norm(residual, ffn_gain)
    piece = ring_gather(mixed, "dp").reshape(dp_size * tok_count, width)
    gated = jnp.dot(piece, w_shared_gate, preferred_element_type=jnp.float32)
    lifted = jnp.dot(piece, w_shared_up, preferred_element_type=jnp.float32)
    hidden = (jax.nn.silu(gated) * lifted).astype(jnp.bfloat16)
    shared_part = (
        jnp.dot(hidden, w_shared_down, preferred_element_type=jnp.float32)
        .astype(jnp.bfloat16)
        .reshape(dp_size, tok_count, width)
    )
    expert_count = w_router.shape[1]
    planes = lax.axis_size("zc")
    plane = lax.axis_index("zc")
    capacity = 4 * tok_count * TOP // (3 * expert_count)
    depth = planes * capacity
    slots = dp_size * depth
    mixed_g = lax.all_gather(mixed, "zc", axis=0, tiled=True)
    mixed_g, shared_part = lax.optimization_barrier((mixed_g, shared_part))
    routes_rel = ring_gather(routes[0], "zc")
    routes_g = jnp.take(routes_rel, (plane - jnp.arange(planes, dtype=jnp.int32)) % planes, axis=0)
    routes_g = routes_g.reshape(planes * tok_count, TOP)
    rows_g = mixed_g.shape[0]
    labels = jnp.arange(expert_count, dtype=jnp.int32)
    logits = jnp.dot(mixed_g, w_router, preferred_element_type=jnp.float32)
    chosen = jnp.sum(
        jnp.where(routes_g[:, :, None] == labels[None, None, :], logits[:, None, :], 0.0), axis=2
    )
    highest = jnp.max(chosen, axis=1, keepdims=True)
    expo = jnp.exp(chosen - highest)
    gates = expo / jnp.sum(expo, axis=1, keepdims=True)
    route_flat = routes_g.reshape(-1)
    inside = (route_flat % planes) == plane
    dest = (route_flat // planes - me_dp) % dp_size
    onehot = ((dest[:, None] == jnp.arange(dp_size, dtype=jnp.int32)[None, :]) & inside[:, None]).astype(jnp.int32)
    slot = jnp.sum(jnp.cumsum(onehot, axis=0) * onehot, axis=1) - 1
    target = jnp.where(inside, dest * depth + slot, -1).reshape(rows_g, TOP)
    hit = target[:, :, None] == jnp.arange(slots, dtype=jnp.int32)[None, None, :]
    placed = jnp.any(hit, axis=1).astype(jnp.bfloat16)
    send = lax.dot_general(
        placed, mixed_g, (((0,), (0,)), ((), ())), preferred_element_type=jnp.float32
    ).astype(jnp.bfloat16)
    send = send.reshape(dp_size, depth, width)
    swap = [(0, 1), (1, 0)]
    returned = []
    for s in range(dp_size):
        mine = send[0] if s == 0 else shifted(send[s], "dp", dp_size, s)
        other = lax.ppermute(mine, "core", swap)
        half_rows = expert_rows(
            jnp.concatenate([mine, other], axis=0), w_expert_gate, w_expert_up, w_expert_down
        )
        from_partner = lax.ppermute(half_rows[depth:], "core", swap)
        expert_out = (
            half_rows[:depth].astype(jnp.float32) + from_partner.astype(jnp.float32)
        ).astype(jnp.bfloat16)
        returned.append(
            expert_out if s == 0 else shifted(expert_out, "dp", dp_size, dp_size - s)
        )
    back = jnp.concatenate(returned, axis=0)
    comb = jnp.sum(jnp.where(hit, gates[:, :, None], 0.0), axis=1)
    first = comb.astype(jnp.bfloat16)
    rest = comb - first.astype(jnp.float32)
    second = rest.astype(jnp.bfloat16)
    third = (rest - second.astype(jnp.float32)).astype(jnp.bfloat16)
    partial = (
        jnp.dot(first, back, preferred_element_type=jnp.float32)
        + jnp.dot(second, back, preferred_element_type=jnp.float32)
        + jnp.dot(third, back, preferred_element_type=jnp.float32)
    )
    routed = lax.psum_scatter(
        partial.astype(jnp.bfloat16), "zc", scatter_dimension=0, tiled=True
    ).astype(jnp.float32)
    shared_sum = ring_scatter(shared_part, "dp")
    output = (residual.astype(jnp.float32) + shared_sum + routed).astype(jnp.bfloat16)
    return output[None]


def solution(mesh):
    dp_size = mesh.shape["dp"]
    planes = mesh.shape["expert"] // 2
    fine = jax.sharding.Mesh(mesh.devices.reshape(dp_size, planes, 2), ("dp", "zc", "core"))
    ex = ("zc", "core")
    in_specs = (
        P(ex, "dp", None),
        P(ex, "dp"),
        P(ex, "dp", None),
        P(),
        P(None, "dp"),
        P(None, "dp"),
        P(None, "dp"),
        P("dp", None),
        P(),
        P(),
        P(None, "dp"),
        P(None, "dp"),
        P("dp", None),
        P(None, ("dp",) + ex),
        P(None, ("dp",) + ex),
        P(("dp",) + ex, None),
    )
    out_specs = P(ex, "dp", None)
    return jax.shard_map(
        per_device, mesh=fine, in_specs=in_specs, out_specs=out_specs, check_vma=False
    )
```

```python
import jax
import jax.numpy as jnp
from jax import lax
from jax.sharding import PartitionSpec as P

HD = 128
TOP = 6


epsilon = 1e-06


def shifted(x, axis, n, s):
    return lax.ppermute(x, axis, [(i, (i + s) % n) for i in range(n)])


def ring_gather(x, axis):
    n = lax.axis_size(axis)
    return jnp.stack([x] + [shifted(x, axis, n, s) for s in range(1, n)])


def ring_scatter(blocks, axis):
    n = lax.axis_size(axis)
    total = blocks[0].astype(jnp.float32)
    for s in range(1, n):
        total = total + shifted(blocks[s], axis, n, n - s).astype(jnp.float32)
    return total


def ring_out(x, axis):
    n = lax.axis_size(axis)
    return jnp.stack([x[0]] + [shifted(x[s], axis, n, s) for s in range(1, n)])


def ring_back(x, axis):
    n = lax.axis_size(axis)
    return jnp.stack([x[0]] + [shifted(x[s], axis, n, n - s) for s in range(1, n)])

def rms_norm(values, gain):
    wide = values.astype(jnp.float32)
    scale = lax.rsqrt(jnp.mean(wide * wide, axis=-1, keepdims=True) + epsilon)
    return (wide * scale * gain).astype(jnp.bfloat16)


def positions(segment, index):
    same = (segment[:, None] == segment[None, :]) & (index[None, :] < index[:, None])
    return jnp.sum(same.astype(jnp.int32), axis=1)


def rotate(heads, place):
    half = heads.shape[-1] // 2
    freq = 10000.0 ** (-jnp.arange(half, dtype=jnp.float32) / half)
    angle = place.astype(jnp.float32)[:, None] * freq[None, :]
    cosine = jnp.cos(angle)[:, None, :]
    sine = jnp.sin(angle)[:, None, :]
    first = heads[..., :half]
    second = heads[..., half:]
    return jnp.concatenate(
        [first * cosine - second * sine, second * cosine + first * sine], axis=-1
    )


def attend(normed, segment, index, w_query, w_key, w_value):
    rows = normed.shape[0]
    query_heads = w_query.shape[1] // HD
    value_heads = w_key.shape[1] // HD
    group_size = query_heads // value_heads
    place = positions(segment, index)
    query = jnp.dot(normed, w_query, preferred_element_type=jnp.float32).reshape(
        rows, query_heads, HD
    )
    query = rotate(query, place).astype(jnp.bfloat16).reshape(rows, value_heads, group_size, HD)
    keyed = jnp.dot(normed, w_key, preferred_element_type=jnp.float32).reshape(
        rows, value_heads, HD
    )
    keyed = rotate(keyed, place).astype(jnp.bfloat16)
    valued = (
        jnp.dot(normed, w_value, preferred_element_type=jnp.float32)
        .astype(jnp.bfloat16)
        .reshape(rows, value_heads, HD)
    )
    block = min(rows, 512)

    def one_block(start):
        index_block = lax.dynamic_slice_in_dim(index, start, block, 0)
        scores = jnp.einsum(
            "qkgd,skd->kgqs", query, keyed, preferred_element_type=jnp.float32
        ) * HD ** (-0.5)
        allowed = (segment[:, None] == segment[None, :]) & (index[None, :] <= index_block[:, None])
        scores = jnp.where(allowed[None, None], scores, -1e30)
        highest = jnp.max(scores, axis=-1, keepdims=True)
        expo = jnp.exp(scores - highest)
        weights = (expo / jnp.sum(expo, axis=-1, keepdims=True)).astype(jnp.bfloat16)
        mixed = jnp.einsum("kgqs,skd->qkgd", weights, valued, preferred_element_type=jnp.float32)
        return mixed.astype(jnp.bfloat16).reshape(block, query_heads * HD)

    if rows == block:
        return one_block(0)
    starts = jnp.arange(rows // block, dtype=jnp.int32) * block
    return lax.map(one_block, starts).reshape(rows, query_heads * HD)


def expert_rows(rows, w_expert_gate, w_expert_up, w_expert_down):
    shape = rows.shape
    flat = rows.reshape(-1, shape[-1])
    gated = jnp.dot(flat, w_expert_gate, preferred_element_type=jnp.float32)
    lifted = jnp.dot(flat, w_expert_up, preferred_element_type=jnp.float32)
    active = (jax.nn.silu(gated) * lifted).astype(jnp.bfloat16)
    return (
        jnp.dot(active, w_expert_down, preferred_element_type=jnp.float32)
        .astype(jnp.bfloat16)
        .reshape(shape)
    )


def per_device(
    tokens,
    segment_ids,
    routes,
    norm_gain,
    w_query,
    w_key,
    w_value,
    w_out,
    ffn_gain,
    w_router,
    w_shared_gate,
    w_shared_up,
    w_shared_down,
    w_expert_gate,
    w_expert_up,
    w_expert_down,
):
    own_rows = tokens[0]
    tok_count = own_rows.shape[0]
    width = own_rows.shape[1]
    normed = rms_norm(own_rows, norm_gain)
    dp_size = lax.axis_size("dp")
    me_dp = lax.axis_index("dp")
    group_rows = ring_gather(normed, "dp").reshape(dp_size * tok_count, width)
    group_segments = ring_gather(segment_ids[0], "dp").reshape(-1)
    home = (me_dp - jnp.arange(dp_size, dtype=jnp.int32)) % dp_size
    group_index = (home[:, None] * tok_count + jnp.arange(tok_count, dtype=jnp.int32)[None, :]).reshape(-1)
    attended = attend(group_rows, group_segments, group_index, w_query, w_key, w_value)
    head_sum = ring_scatter(
        jnp.dot(attended, w_out, preferred_element_type=jnp.float32)
        .astype(jnp.bfloat16)
        .reshape(dp_size, tok_count, width),
        "dp",
    )
    residual = (own_rows.astype(jnp.float32) + head_sum).astype(jnp.bfloat16)
    mixed = rms_norm(residual, ffn_gain)
    piece = ring_gather(mixed, "dp").reshape(dp_size * tok_count, width)
    gated = jnp.dot(piece, w_shared_gate, preferred_element_type=jnp.float32)
    lifted = jnp.dot(piece, w_shared_up, preferred_element_type=jnp.float32)
    hidden = (jax.nn.silu(gated) * lifted).astype(jnp.bfloat16)
    shared_part = (
        jnp.dot(hidden, w_shared_down, preferred_element_type=jnp.float32)
        .astype(jnp.bfloat16)
        .reshape(dp_size, tok_count, width)
    )
    expert_count = w_router.shape[1]
    planes = lax.axis_size("zc")
    plane = lax.axis_index("zc")
    capacity = 4 * tok_count * TOP // (3 * expert_count)
    depth = planes * capacity
    slots = dp_size * depth
    mixed_g = lax.all_gather(mixed, "zc", axis=0, tiled=True)
    mixed_g, shared_part = lax.optimization_barrier((mixed_g, shared_part))
    routes_rel = ring_gather(routes[0], "zc")
    routes_g = jnp.take(routes_rel, (plane - jnp.arange(planes, dtype=jnp.int32)) % planes, axis=0)
    routes_g = routes_g.reshape(planes * tok_count, TOP)
    rows_g = mixed_g.shape[0]
    labels = jnp.arange(expert_count, dtype=jnp.int32)
    logits = jnp.dot(mixed_g, w_router, preferred_element_type=jnp.float32)
    chosen = jnp.sum(
        jnp.where(routes_g[:, :, None] == labels[None, None, :], logits[:, None, :], 0.0), axis=2
    )
    highest = jnp.max(chosen, axis=1, keepdims=True)
    expo = jnp.exp(chosen - highest)
    gates = expo / jnp.sum(expo, axis=1, keepdims=True)
    route_flat = routes_g.reshape(-1)
    inside = (route_flat % planes) == plane
    dest = (route_flat // planes - me_dp) % dp_size
    onehot = ((dest[:, None] == jnp.arange(dp_size, dtype=jnp.int32)[None, :]) & inside[:, None]).astype(jnp.int32)
    slot = jnp.sum(jnp.cumsum(onehot, axis=0) * onehot, axis=1) - 1
    target = jnp.where(inside, dest * depth + slot, -1).reshape(rows_g, TOP)
    hit = target[:, :, None] == jnp.arange(slots, dtype=jnp.int32)[None, None, :]
    placed = jnp.any(hit, axis=1).astype(jnp.bfloat16)
    send = lax.dot_general(
        placed, mixed_g, (((0,), (0,)), ((), ())), preferred_element_type=jnp.float32
    ).astype(jnp.bfloat16)
    comb = jnp.sum(jnp.where(hit, gates[:, :, None], 0.0), axis=1)
    first = comb.astype(jnp.bfloat16)
    rest = comb - first.astype(jnp.float32)
    second = rest.astype(jnp.bfloat16)
    third = (rest - second.astype(jnp.float32)).astype(jnp.bfloat16)
    pieces = jnp.concatenate([first, second, third], axis=0)
    recv = ring_out(send.reshape(dp_size, depth, width), "dp")
    recv, pieces = lax.optimization_barrier((recv, pieces))
    mine = recv.reshape(slots, width)
    swap = [(0, 1), (1, 0)]
    other = lax.ppermute(mine, "core", swap)
    half_rows = expert_rows(
        jnp.concatenate([mine, other], axis=0), w_expert_gate, w_expert_up, w_expert_down
    )
    from_partner = lax.ppermute(half_rows[slots:], "core", swap)
    expert_out = (
        half_rows[:slots].astype(jnp.float32) + from_partner.astype(jnp.float32)
    ).astype(jnp.bfloat16)
    back = ring_back(expert_out.reshape(dp_size, depth, width), "dp").reshape(slots, width)
    partial = jnp.sum(
        jnp.dot(pieces, back, preferred_element_type=jnp.float32).reshape(3, rows_g, width), axis=0
    )
    routed = lax.psum_scatter(
        partial.astype(jnp.bfloat16), "zc", scatter_dimension=0, tiled=True
    ).astype(jnp.float32)
    shared_sum = ring_scatter(shared_part, "dp")
    output = (residual.astype(jnp.float32) + shared_sum + routed).astype(jnp.bfloat16)
    return output[None]


def solution(mesh):
    dp_size = mesh.shape["dp"]
    planes = mesh.shape["expert"] // 2
    fine = jax.sharding.Mesh(mesh.devices.reshape(dp_size, planes, 2), ("dp", "zc", "core"))
    ex = ("zc", "core")
    in_specs = (
        P(ex, "dp", None),
        P(ex, "dp"),
        P(ex, "dp", None),
        P(),
        P(None, "dp"),
        P(None, "dp"),
        P(None, "dp"),
        P("dp", None),
        P(),
        P(),
        P(None, "dp"),
        P(None, "dp"),
        P("dp", None),
        P(None, ("dp",) + ex),
        P(None, ("dp",) + ex),
        P(("dp",) + ex, None),
    )
    out_specs = P(ex, "dp", None)
    return jax.shard_map(
        per_device, mesh=fine, in_specs=in_specs, out_specs=out_specs, check_vma=False
    )
```

```python
import jax
import jax.numpy as jnp
from jax import lax
from jax.sharding import PartitionSpec as P

HD = 128
TOP = 6


epsilon = 1e-06


def shifted(x, axis, n, s):
    return lax.ppermute(x, axis, [(i, (i + s) % n) for i in range(n)])


def ring_gather(x, axis):
    n = lax.axis_size(axis)
    return jnp.stack([x] + [shifted(x, axis, n, s) for s in range(1, n)])


def ring_scatter(blocks, axis):
    n = lax.axis_size(axis)
    total = blocks[0].astype(jnp.float32)
    for s in range(1, n):
        total = total + shifted(blocks[s], axis, n, n - s).astype(jnp.float32)
    return total


def ring_out(x, axis):
    n = lax.axis_size(axis)
    return jnp.stack([x[0]] + [shifted(x[s], axis, n, s) for s in range(1, n)])


def ring_back(x, axis):
    n = lax.axis_size(axis)
    return jnp.stack([x[0]] + [shifted(x[s], axis, n, n - s) for s in range(1, n)])

def rms_norm(values, gain):
    wide = values.astype(jnp.float32)
    scale = lax.rsqrt(jnp.mean(wide * wide, axis=-1, keepdims=True) + epsilon)
    return (wide * scale * gain).astype(jnp.bfloat16)


def positions(segment, index):
    same = (segment[:, None] == segment[None, :]) & (index[None, :] < index[:, None])
    return jnp.sum(same.astype(jnp.int32), axis=1)


def rotate(heads, place):
    half = heads.shape[-1] // 2
    freq = 10000.0 ** (-jnp.arange(half, dtype=jnp.float32) / half)
    angle = place.astype(jnp.float32)[:, None] * freq[None, :]
    cosine = jnp.cos(angle)[:, None, :]
    sine = jnp.sin(angle)[:, None, :]
    first = heads[..., :half]
    second = heads[..., half:]
    return jnp.concatenate(
        [first * cosine - second * sine, second * cosine + first * sine], axis=-1
    )


def attend(normed, segment, index, w_query, w_key, w_value):
    rows = normed.shape[0]
    query_heads = w_query.shape[1] // HD
    value_heads = w_key.shape[1] // HD
    group_size = query_heads // value_heads
    place = positions(segment, index)
    query = jnp.dot(normed, w_query, preferred_element_type=jnp.float32).reshape(
        rows, query_heads, HD
    )
    query = rotate(query, place).astype(jnp.bfloat16).reshape(rows, value_heads, group_size, HD)
    keyed = jnp.dot(normed, w_key, preferred_element_type=jnp.float32).reshape(
        rows, value_heads, HD
    )
    keyed = rotate(keyed, place).astype(jnp.bfloat16)
    valued = (
        jnp.dot(normed, w_value, preferred_element_type=jnp.float32)
        .astype(jnp.bfloat16)
        .reshape(rows, value_heads, HD)
    )
    block = min(rows, 512)

    def one_block(start):
        index_block = lax.dynamic_slice_in_dim(index, start, block, 0)
        scores = jnp.einsum(
            "qkgd,skd->kgqs", query, keyed, preferred_element_type=jnp.float32
        ) * HD ** (-0.5)
        allowed = (segment[:, None] == segment[None, :]) & (index[None, :] <= index_block[:, None])
        scores = jnp.where(allowed[None, None], scores, -1e30)
        highest = jnp.max(scores, axis=-1, keepdims=True)
        expo = jnp.exp(scores - highest)
        weights = (expo / jnp.sum(expo, axis=-1, keepdims=True)).astype(jnp.bfloat16)
        mixed = jnp.einsum("kgqs,skd->qkgd", weights, valued, preferred_element_type=jnp.float32)
        return mixed.astype(jnp.bfloat16).reshape(block, query_heads * HD)

    starts = jnp.arange(rows // block, dtype=jnp.int32) * block
    return lax.map(one_block, starts).reshape(rows, query_heads * HD)


def expert_rows(rows, w_expert_gate, w_expert_up, w_expert_down):
    shape = rows.shape
    flat = rows.reshape(-1, shape[-1])
    gated = jnp.dot(flat, w_expert_gate, preferred_element_type=jnp.float32)
    lifted = jnp.dot(flat, w_expert_up, preferred_element_type=jnp.float32)
    active = (jax.nn.silu(gated) * lifted).astype(jnp.bfloat16)
    return (
        jnp.dot(active, w_expert_down, preferred_element_type=jnp.float32)
        .astype(jnp.bfloat16)
        .reshape(shape)
    )


def per_device(
    tokens,
    segment_ids,
    routes,
    norm_gain,
    w_query,
    w_key,
    w_value,
    w_out,
    ffn_gain,
    w_router,
    w_shared_gate,
    w_shared_up,
    w_shared_down,
    w_expert_gate,
    w_expert_up,
    w_expert_down,
):
    own_rows = tokens[0]
    tok_count = own_rows.shape[0]
    width = own_rows.shape[1]
    normed = rms_norm(own_rows, norm_gain)
    dp_size = lax.axis_size("dp")
    me_dp = lax.axis_index("dp")
    group_rows = ring_gather(normed, "dp").reshape(dp_size * tok_count, width)
    group_segments = ring_gather(segment_ids[0], "dp").reshape(-1)
    home = (me_dp - jnp.arange(dp_size, dtype=jnp.int32)) % dp_size
    group_index = (home[:, None] * tok_count + jnp.arange(tok_count, dtype=jnp.int32)[None, :]).reshape(-1)
    attended = attend(group_rows, group_segments, group_index, w_query, w_key, w_value)
    head_sum = ring_scatter(
        jnp.dot(attended, w_out, preferred_element_type=jnp.float32)
        .astype(jnp.bfloat16)
        .reshape(dp_size, tok_count, width),
        "dp",
    )
    residual = (own_rows.astype(jnp.float32) + head_sum).astype(jnp.bfloat16)
    mixed = rms_norm(residual, ffn_gain)
    piece = ring_gather(mixed, "dp").reshape(dp_size * tok_count, width)
    gated = jnp.dot(piece, w_shared_gate, preferred_element_type=jnp.float32)
    lifted = jnp.dot(piece, w_shared_up, preferred_element_type=jnp.float32)
    hidden = (jax.nn.silu(gated) * lifted).astype(jnp.bfloat16)
    shared_part = (
        jnp.dot(hidden, w_shared_down, preferred_element_type=jnp.float32)
        .astype(jnp.bfloat16)
        .reshape(dp_size, tok_count, width)
    )
    expert_count = w_router.shape[1]
    planes = lax.axis_size("zc")
    plane = lax.axis_index("zc")
    capacity = 4 * tok_count * TOP // (3 * expert_count)
    depth = (planes - 1) * capacity
    slots = dp_size * depth
    mixed_g = lax.all_gather(mixed, "zc", axis=0, tiled=True)
    mixed_g, shared_part = lax.optimization_barrier((mixed_g, shared_part))
    routes_rel = ring_gather(routes[0], "zc")
    routes_g = jnp.take(routes_rel, (plane - jnp.arange(planes, dtype=jnp.int32)) % planes, axis=0)
    routes_g = routes_g.reshape(planes * tok_count, TOP)
    rows_g = mixed_g.shape[0]
    labels = jnp.arange(expert_count, dtype=jnp.int32)
    logits = jnp.dot(mixed_g, w_router, preferred_element_type=jnp.float32)
    chosen = jnp.sum(
        jnp.where(routes_g[:, :, None] == labels[None, None, :], logits[:, None, :], 0.0), axis=2
    )
    highest = jnp.max(chosen, axis=1, keepdims=True)
    expo = jnp.exp(chosen - highest)
    gates = expo / jnp.sum(expo, axis=1, keepdims=True)
    route_flat = routes_g.reshape(-1)
    block_of = (jnp.arange(rows_g * TOP, dtype=jnp.int32) // TOP) // tok_count
    inside = ((route_flat % planes) == plane) & (block_of != plane)
    dest = (route_flat // planes - me_dp) % dp_size
    onehot = ((dest[:, None] == jnp.arange(dp_size, dtype=jnp.int32)[None, :]) & inside[:, None]).astype(jnp.int32)
    slot = jnp.sum(jnp.cumsum(onehot, axis=0) * onehot, axis=1) - 1
    target = jnp.where(inside, dest * depth + slot, -1).reshape(rows_g, TOP)
    hit = target[:, :, None] == jnp.arange(slots, dtype=jnp.int32)[None, None, :]
    placed = jnp.any(hit, axis=1).astype(jnp.bfloat16)
    send = lax.dot_general(
        placed, mixed_g, (((0,), (0,)), ((), ())), preferred_element_type=jnp.float32
    ).astype(jnp.bfloat16)
    recv = ring_out(send.reshape(dp_size, depth, width), "dp")
    rows_p = piece.shape[0]
    routes_p = ring_gather(routes[0], "dp").reshape(rows_p, TOP)
    logits_p = jnp.dot(piece, w_router, preferred_element_type=jnp.float32)
    chosen_p = jnp.sum(
        jnp.where(routes_p[:, :, None] == labels[None, None, :], logits_p[:, None, :], 0.0), axis=2
    )
    expo_p = jnp.exp(chosen_p - jnp.max(chosen_p, axis=1, keepdims=True))
    gates_p = expo_p / jnp.sum(expo_p, axis=1, keepdims=True)
    local_depth = dp_size * capacity
    own_p = (routes_p.reshape(-1) == me_dp * planes + plane).astype(jnp.int32)
    target_p = jnp.where(own_p > 0, jnp.cumsum(own_p) - 1, -1).reshape(rows_p, TOP)
    hit_p = target_p[:, :, None] == jnp.arange(local_depth, dtype=jnp.int32)[None, None, :]
    local_rows = lax.dot_general(
        jnp.any(hit_p, axis=1).astype(jnp.bfloat16),
        piece,
        (((0,), (0,)), ((), ())),
        preferred_element_type=jnp.float32,
    ).astype(jnp.bfloat16)
    mine = jnp.concatenate([recv.reshape(slots, width), local_rows], axis=0)
    swap = [(0, 1), (1, 0)]
    other = lax.ppermute(mine, "core", swap)
    half_rows = expert_rows(
        jnp.concatenate([mine, other], axis=0), w_expert_gate, w_expert_up, w_expert_down
    )
    held = slots + local_depth
    from_partner = lax.ppermute(half_rows[held:], "core", swap)
    expert_all = (
        half_rows[:held].astype(jnp.float32) + from_partner.astype(jnp.float32)
    ).astype(jnp.bfloat16)
    expert_out = expert_all[:slots]
    back = ring_back(expert_out.reshape(dp_size, depth, width), "dp").reshape(slots, width)
    comb_p = jnp.sum(jnp.where(hit_p, gates_p[:, :, None], 0.0), axis=1)
    first_p = comb_p.astype(jnp.bfloat16)
    rest_p = comb_p - first_p.astype(jnp.float32)
    second_p = rest_p.astype(jnp.bfloat16)
    third_p = (rest_p - second_p.astype(jnp.float32)).astype(jnp.bfloat16)
    local_out = expert_all[slots:]
    routed_p = (
        jnp.dot(first_p, local_out, preferred_element_type=jnp.float32)
        + jnp.dot(second_p, local_out, preferred_element_type=jnp.float32)
        + jnp.dot(third_p, local_out, preferred_element_type=jnp.float32)
    )
    shared_send = (
        shared_part.astype(jnp.float32) + routed_p.reshape(dp_size, tok_count, width)
    ).astype(jnp.bfloat16)
    comb = jnp.sum(jnp.where(hit, gates[:, :, None], 0.0), axis=1)
    first = comb.astype(jnp.bfloat16)
    rest = comb - first.astype(jnp.float32)
    second = rest.astype(jnp.bfloat16)
    third = (rest - second.astype(jnp.float32)).astype(jnp.bfloat16)
    partial = (
        jnp.dot(first, back, preferred_element_type=jnp.float32)
        + jnp.dot(second, back, preferred_element_type=jnp.float32)
        + jnp.dot(third, back, preferred_element_type=jnp.float32)
    )
    routed = lax.psum_scatter(
        partial.astype(jnp.bfloat16), "zc", scatter_dimension=0, tiled=True
    ).astype(jnp.float32)
    shared_sum = ring_scatter(shared_send, "dp")
    output = (residual.astype(jnp.float32) + shared_sum + routed).astype(jnp.bfloat16)
    return output[None]


def solution(mesh):
    dp_size = mesh.shape["dp"]
    planes = mesh.shape["expert"] // 2
    fine = jax.sharding.Mesh(mesh.devices.reshape(dp_size, planes, 2), ("dp", "zc", "core"))
    ex = ("zc", "core")
    in_specs = (
        P(ex, "dp", None),
        P(ex, "dp"),
        P(ex, "dp", None),
        P(),
        P(None, "dp"),
        P(None, "dp"),
        P(None, "dp"),
        P("dp", None),
        P(),
        P(),
        P(None, "dp"),
        P(None, "dp"),
        P("dp", None),
        P(None, ("dp",) + ex),
        P(None, ("dp",) + ex),
        P(("dp",) + ex, None),
    )
    out_specs = P(ex, "dp", None)
    return jax.shard_map(
        per_device, mesh=fine, in_specs=in_specs, out_specs=out_specs, check_vma=False
    )
```

```python
import jax
import jax.numpy as jnp
from jax import lax
from jax.sharding import PartitionSpec as P

HD = 128
TOP = 6


epsilon = 1e-06


def shifted(x, axis, n, s):
    return lax.ppermute(x, axis, [(i, (i + s) % n) for i in range(n)])


def ring_gather(x, axis):
    n = lax.axis_size(axis)
    return jnp.stack([x] + [shifted(x, axis, n, s) for s in range(1, n)])


def ring_scatter(blocks, axis):
    n = lax.axis_size(axis)
    total = blocks[0].astype(jnp.float32)
    for s in range(1, n):
        total = total + shifted(blocks[s], axis, n, n - s).astype(jnp.float32)
    return total


def ring_out(x, axis):
    n = lax.axis_size(axis)
    return jnp.stack([x[0]] + [shifted(x[s], axis, n, s) for s in range(1, n)])


def ring_back(x, axis):
    n = lax.axis_size(axis)
    return jnp.stack([x[0]] + [shifted(x[s], axis, n, n - s) for s in range(1, n)])

def rms_norm(values, gain):
    wide = values.astype(jnp.float32)
    scale = lax.rsqrt(jnp.mean(wide * wide, axis=-1, keepdims=True) + epsilon)
    return (wide * scale * gain).astype(jnp.bfloat16)


def positions(segment, index):
    same = (segment[:, None] == segment[None, :]) & (index[None, :] < index[:, None])
    return jnp.sum(same.astype(jnp.int32), axis=1)


def rotate(heads, place):
    half = heads.shape[-1] // 2
    freq = 10000.0 ** (-jnp.arange(half, dtype=jnp.float32) / half)
    angle = place.astype(jnp.float32)[:, None] * freq[None, :]
    cosine = jnp.cos(angle)[:, None, :]
    sine = jnp.sin(angle)[:, None, :]
    first = heads[..., :half]
    second = heads[..., half:]
    return jnp.concatenate(
        [first * cosine - second * sine, second * cosine + first * sine], axis=-1
    )


def attend(normed, segment, index, w_query, w_key, w_value):
    rows = normed.shape[0]
    query_heads = w_query.shape[1] // HD
    value_heads = w_key.shape[1] // HD
    group_size = query_heads // value_heads
    place = positions(segment, index)
    query = jnp.dot(normed, w_query, preferred_element_type=jnp.float32).reshape(
        rows, query_heads, HD
    )
    query = rotate(query, place).astype(jnp.bfloat16).reshape(rows, value_heads, group_size, HD)
    keyed = jnp.dot(normed, w_key, preferred_element_type=jnp.float32).reshape(
        rows, value_heads, HD
    )
    keyed = rotate(keyed, place).astype(jnp.bfloat16)
    valued = (
        jnp.dot(normed, w_value, preferred_element_type=jnp.float32)
        .astype(jnp.bfloat16)
        .reshape(rows, value_heads, HD)
    )
    block = min(rows, 512)

    def one_block(start):
        index_block = lax.dynamic_slice_in_dim(index, start, block, 0)
        scores = jnp.einsum(
            "qkgd,skd->kgqs", query, keyed, preferred_element_type=jnp.float32
        ) * HD ** (-0.5)
        allowed = (segment[:, None] == segment[None, :]) & (index[None, :] <= index_block[:, None])
        scores = jnp.where(allowed[None, None], scores, -1e30)
        highest = jnp.max(scores, axis=-1, keepdims=True)
        expo = jnp.exp(scores - highest)
        weights = (expo / jnp.sum(expo, axis=-1, keepdims=True)).astype(jnp.bfloat16)
        mixed = jnp.einsum("kgqs,skd->qkgd", weights, valued, preferred_element_type=jnp.float32)
        return mixed.astype(jnp.bfloat16).reshape(block, query_heads * HD)

    starts = jnp.arange(rows // block, dtype=jnp.int32) * block
    return lax.map(one_block, starts).reshape(rows, query_heads * HD)


def expert_rows(rows, w_expert_gate, w_expert_up, w_expert_down):
    shape = rows.shape
    flat = rows.reshape(-1, shape[-1])
    gated = jnp.dot(flat, w_expert_gate, preferred_element_type=jnp.float32)
    lifted = jnp.dot(flat, w_expert_up, preferred_element_type=jnp.float32)
    active = (jax.nn.silu(gated) * lifted).astype(jnp.bfloat16)
    return (
        jnp.dot(active, w_expert_down, preferred_element_type=jnp.float32)
        .astype(jnp.bfloat16)
        .reshape(shape)
    )


def per_device(
    tokens,
    segment_ids,
    routes,
    norm_gain,
    w_query,
    w_key,
    w_value,
    w_out,
    ffn_gain,
    w_router,
    w_shared_gate,
    w_shared_up,
    w_shared_down,
    w_expert_gate,
    w_expert_up,
    w_expert_down,
):
    own_rows = tokens[0]
    tok_count = own_rows.shape[0]
    width = own_rows.shape[1]
    normed = rms_norm(own_rows, norm_gain)
    dp_size = lax.axis_size("dp")
    me_dp = lax.axis_index("dp")
    group_rows = ring_gather(normed, "dp").reshape(dp_size * tok_count, width)
    group_segments = ring_gather(segment_ids[0], "dp").reshape(-1)
    home = (me_dp - jnp.arange(dp_size, dtype=jnp.int32)) % dp_size
    group_index = (home[:, None] * tok_count + jnp.arange(tok_count, dtype=jnp.int32)[None, :]).reshape(-1)
    attended = attend(group_rows, group_segments, group_index, w_query, w_key, w_value)
    head_sum = ring_scatter(
        jnp.dot(attended, w_out, preferred_element_type=jnp.float32)
        .astype(jnp.bfloat16)
        .reshape(dp_size, tok_count, width),
        "dp",
    )
    residual = (own_rows.astype(jnp.float32) + head_sum).astype(jnp.bfloat16)
    mixed = rms_norm(residual, ffn_gain)
    piece = ring_gather(mixed, "dp").reshape(dp_size * tok_count, width)
    gated = jnp.dot(piece, w_shared_gate, preferred_element_type=jnp.float32)
    lifted = jnp.dot(piece, w_shared_up, preferred_element_type=jnp.float32)
    hidden = (jax.nn.silu(gated) * lifted).astype(jnp.bfloat16)
    shared_part = (
        jnp.dot(hidden, w_shared_down, preferred_element_type=jnp.float32)
        .astype(jnp.bfloat16)
        .reshape(dp_size, tok_count, width)
    )
    expert_count = w_router.shape[1]
    planes = lax.axis_size("zc")
    plane = lax.axis_index("zc")
    capacity = 4 * tok_count * TOP // (3 * expert_count)
    depth = (planes - 1) * capacity
    slots = dp_size * depth
    mixed_g = lax.all_gather(mixed, "zc", axis=0, tiled=True)
    mixed_g, shared_part = lax.optimization_barrier((mixed_g, shared_part))
    routes_rel = ring_gather(routes[0], "zc")
    routes_g = jnp.take(routes_rel, (plane - jnp.arange(planes, dtype=jnp.int32)) % planes, axis=0)
    routes_g = routes_g.reshape(planes * tok_count, TOP)
    rows_g = mixed_g.shape[0]
    labels = jnp.arange(expert_count, dtype=jnp.int32)
    logits = jnp.dot(mixed_g, w_router, preferred_element_type=jnp.float32)
    chosen = jnp.sum(
        jnp.where(routes_g[:, :, None] == labels[None, None, :], logits[:, None, :], 0.0), axis=2
    )
    highest = jnp.max(chosen, axis=1, keepdims=True)
    expo = jnp.exp(chosen - highest)
    gates = expo / jnp.sum(expo, axis=1, keepdims=True)
    route_flat = routes_g.reshape(-1)
    block_of = (jnp.arange(rows_g * TOP, dtype=jnp.int32) // TOP) // tok_count
    inside = ((route_flat % planes) == plane) & (block_of != plane)
    dest = (route_flat // planes - me_dp) % dp_size
    onehot = ((dest[:, None] == jnp.arange(dp_size, dtype=jnp.int32)[None, :]) & inside[:, None]).astype(jnp.int32)
    slot = jnp.sum(jnp.cumsum(onehot, axis=0) * onehot, axis=1) - 1
    target = jnp.where(inside, dest * depth + slot, -1).reshape(rows_g, TOP)
    hit = target[:, :, None] == jnp.arange(slots, dtype=jnp.int32)[None, None, :]
    placed = jnp.any(hit, axis=1).astype(jnp.bfloat16)
    send = lax.dot_general(
        placed, mixed_g, (((0,), (0,)), ((), ())), preferred_element_type=jnp.float32
    ).astype(jnp.bfloat16)
    recv = ring_out(send.reshape(dp_size, depth, width), "dp")
    rows_p = piece.shape[0]
    routes_p = ring_gather(routes[0], "dp").reshape(rows_p, TOP)
    logits_p = jnp.dot(piece, w_router, preferred_element_type=jnp.float32)
    chosen_p = jnp.sum(
        jnp.where(routes_p[:, :, None] == labels[None, None, :], logits_p[:, None, :], 0.0), axis=2
    )
    expo_p = jnp.exp(chosen_p - jnp.max(chosen_p, axis=1, keepdims=True))
    gates_p = expo_p / jnp.sum(expo_p, axis=1, keepdims=True)
    local_depth = dp_size * capacity
    own_p = (routes_p.reshape(-1) == me_dp * planes + plane).astype(jnp.int32)
    target_p = jnp.where(own_p > 0, jnp.cumsum(own_p) - 1, -1).reshape(rows_p, TOP)
    hit_p = target_p[:, :, None] == jnp.arange(local_depth, dtype=jnp.int32)[None, None, :]
    local_rows = lax.dot_general(
        jnp.any(hit_p, axis=1).astype(jnp.bfloat16),
        piece,
        (((0,), (0,)), ((), ())),
        preferred_element_type=jnp.float32,
    ).astype(jnp.bfloat16)
    mine = jnp.concatenate([recv.reshape(slots, width), local_rows], axis=0)
    swap = [(0, 1), (1, 0)]
    other = lax.ppermute(mine, "core", swap)
    half_rows = expert_rows(
        jnp.concatenate([mine, other], axis=0), w_expert_gate, w_expert_up, w_expert_down
    )
    held = slots + local_depth
    from_partner = lax.ppermute(half_rows[held:], "core", swap)
    expert_all = (
        half_rows[:held].astype(jnp.float32) + from_partner.astype(jnp.float32)
    ).astype(jnp.bfloat16)
    expert_out = expert_all[:slots]
    comb_p = jnp.sum(jnp.where(hit_p, gates_p[:, :, None], 0.0), axis=1)
    first_p = comb_p.astype(jnp.bfloat16)
    rest_p = comb_p - first_p.astype(jnp.float32)
    second_p = rest_p.astype(jnp.bfloat16)
    third_p = (rest_p - second_p.astype(jnp.float32)).astype(jnp.bfloat16)
    local_out = expert_all[slots:]
    routed_p = (
        jnp.dot(first_p, local_out, preferred_element_type=jnp.float32)
        + jnp.dot(second_p, local_out, preferred_element_type=jnp.float32)
        + jnp.dot(third_p, local_out, preferred_element_type=jnp.float32)
    )
    shared_send = (
        shared_part.astype(jnp.float32) + routed_p.reshape(dp_size, tok_count, width)
    ).astype(jnp.bfloat16)
    expert_out, shared_send = lax.optimization_barrier((expert_out, shared_send))
    back = ring_back(expert_out.reshape(dp_size, depth, width), "dp").reshape(slots, width)
    comb = jnp.sum(jnp.where(hit, gates[:, :, None], 0.0), axis=1)
    first = comb.astype(jnp.bfloat16)
    rest = comb - first.astype(jnp.float32)
    second = rest.astype(jnp.bfloat16)
    third = (rest - second.astype(jnp.float32)).astype(jnp.bfloat16)
    partial = (
        jnp.dot(first, back, preferred_element_type=jnp.float32)
        + jnp.dot(second, back, preferred_element_type=jnp.float32)
        + jnp.dot(third, back, preferred_element_type=jnp.float32)
    )
    routed = lax.psum_scatter(
        partial.astype(jnp.bfloat16), "zc", scatter_dimension=0, tiled=True
    ).astype(jnp.float32)
    shared_sum = ring_scatter(shared_send, "dp")
    output = (residual.astype(jnp.float32) + shared_sum + routed).astype(jnp.bfloat16)
    return output[None]


def solution(mesh):
    dp_size = mesh.shape["dp"]
    planes = mesh.shape["expert"] // 2
    fine = jax.sharding.Mesh(mesh.devices.reshape(dp_size, planes, 2), ("dp", "zc", "core"))
    ex = ("zc", "core")
    in_specs = (
        P(ex, "dp", None),
        P(ex, "dp"),
        P(ex, "dp", None),
        P(),
        P(None, "dp"),
        P(None, "dp"),
        P(None, "dp"),
        P("dp", None),
        P(),
        P(),
        P(None, "dp"),
        P(None, "dp"),
        P("dp", None),
        P(None, ("dp",) + ex),
        P(None, ("dp",) + ex),
        P(("dp",) + ex, None),
    )
    out_specs = P(ex, "dp", None)
    return jax.shard_map(
        per_device, mesh=fine, in_specs=in_specs, out_specs=out_specs, check_vma=False
    )
```

```python
import jax
import jax.numpy as jnp
from jax import lax
from jax.sharding import PartitionSpec as P

HD = 128
TOP = 6


epsilon = 1e-06


def shifted(x, axis, n, s):
    return lax.ppermute(x, axis, [(i, (i + s) % n) for i in range(n)])


def ring_gather(x, axis):
    n = lax.axis_size(axis)
    return jnp.stack([x] + [shifted(x, axis, n, s) for s in range(1, n)])


def ring_scatter(blocks, axis):
    n = lax.axis_size(axis)
    total = blocks[0].astype(jnp.float32)
    for s in range(1, n):
        total = total + shifted(blocks[s], axis, n, n - s).astype(jnp.float32)
    return total


def ring_out(x, axis):
    n = lax.axis_size(axis)
    return jnp.stack([x[0]] + [shifted(x[s], axis, n, s) for s in range(1, n)])


def ring_back(x, axis):
    n = lax.axis_size(axis)
    return jnp.stack([x[0]] + [shifted(x[s], axis, n, n - s) for s in range(1, n)])

def rms_norm(values, gain):
    wide = values.astype(jnp.float32)
    scale = lax.rsqrt(jnp.mean(wide * wide, axis=-1, keepdims=True) + epsilon)
    return (wide * scale * gain).astype(jnp.bfloat16)


def positions(segment, index):
    same = (segment[:, None] == segment[None, :]) & (index[None, :] < index[:, None])
    return jnp.sum(same.astype(jnp.int32), axis=1)


def rotate(heads, place):
    half = heads.shape[-1] // 2
    freq = 10000.0 ** (-jnp.arange(half, dtype=jnp.float32) / half)
    angle = place.astype(jnp.float32)[:, None] * freq[None, :]
    cosine = jnp.cos(angle)[:, None, :]
    sine = jnp.sin(angle)[:, None, :]
    first = heads[..., :half]
    second = heads[..., half:]
    return jnp.concatenate(
        [first * cosine - second * sine, second * cosine + first * sine], axis=-1
    )


def attend(normed, segment, index, w_query, w_key, w_value):
    rows = normed.shape[0]
    query_heads = w_query.shape[1] // HD
    value_heads = w_key.shape[1] // HD
    group_size = query_heads // value_heads
    place = positions(segment, index)
    query = jnp.dot(normed, w_query, preferred_element_type=jnp.float32).reshape(
        rows, query_heads, HD
    )
    query = rotate(query, place).astype(jnp.bfloat16).reshape(rows, value_heads, group_size, HD)
    keyed = jnp.dot(normed, w_key, preferred_element_type=jnp.float32).reshape(
        rows, value_heads, HD
    )
    keyed = rotate(keyed, place).astype(jnp.bfloat16)
    valued = (
        jnp.dot(normed, w_value, preferred_element_type=jnp.float32)
        .astype(jnp.bfloat16)
        .reshape(rows, value_heads, HD)
    )
    block = min(rows, 512)

    def one_block(start):
        index_block = lax.dynamic_slice_in_dim(index, start, block, 0)
        scores = jnp.einsum(
            "qkgd,skd->kgqs", query, keyed, preferred_element_type=jnp.float32
        ) * HD ** (-0.5)
        allowed = (segment[:, None] == segment[None, :]) & (index[None, :] <= index_block[:, None])
        scores = jnp.where(allowed[None, None], scores, -1e30)
        highest = jnp.max(scores, axis=-1, keepdims=True)
        expo = jnp.exp(scores - highest)
        weights = (expo / jnp.sum(expo, axis=-1, keepdims=True)).astype(jnp.bfloat16)
        mixed = jnp.einsum("kgqs,skd->qkgd", weights, valued, preferred_element_type=jnp.float32)
        return mixed.astype(jnp.bfloat16).reshape(block, query_heads * HD)

    starts = jnp.arange(rows // block, dtype=jnp.int32) * block
    return lax.map(one_block, starts).reshape(rows, query_heads * HD)


def expert_rows(rows, w_expert_gate, w_expert_up, w_expert_down):
    shape = rows.shape
    flat = rows.reshape(-1, shape[-1])
    gated = jnp.dot(flat, w_expert_gate, preferred_element_type=jnp.float32)
    lifted = jnp.dot(flat, w_expert_up, preferred_element_type=jnp.float32)
    active = (jax.nn.silu(gated) * lifted).astype(jnp.bfloat16)
    return (
        jnp.dot(active, w_expert_down, preferred_element_type=jnp.float32)
        .astype(jnp.bfloat16)
        .reshape(shape)
    )


def per_device(
    tokens,
    segment_ids,
    routes,
    norm_gain,
    w_query,
    w_key,
    w_value,
    w_out,
    ffn_gain,
    w_router,
    w_shared_gate,
    w_shared_up,
    w_shared_down,
    w_expert_gate,
    w_expert_up,
    w_expert_down,
):
    own_rows = tokens[0]
    tok_count = own_rows.shape[0]
    width = own_rows.shape[1]
    normed = rms_norm(own_rows, norm_gain)
    dp_size = lax.axis_size("dp")
    me_dp = lax.axis_index("dp")
    group_rows = ring_gather(normed, "dp").reshape(dp_size * tok_count, width)
    tags = ring_gather(jnp.concatenate([routes[0], segment_ids[0][:, None]], axis=1), "dp")
    group_segments = tags[:, :, TOP].reshape(-1)
    home = (me_dp - jnp.arange(dp_size, dtype=jnp.int32)) % dp_size
    group_index = (home[:, None] * tok_count + jnp.arange(tok_count, dtype=jnp.int32)[None, :]).reshape(-1)
    attended = attend(group_rows, group_segments, group_index, w_query, w_key, w_value)
    head_sum = ring_scatter(
        jnp.dot(attended, w_out, preferred_element_type=jnp.float32)
        .astype(jnp.bfloat16)
        .reshape(dp_size, tok_count, width),
        "dp",
    )
    residual = (own_rows.astype(jnp.float32) + head_sum).astype(jnp.bfloat16)
    mixed = rms_norm(residual, ffn_gain)
    piece = ring_gather(mixed, "dp").reshape(dp_size * tok_count, width)
    gated = jnp.dot(piece, w_shared_gate, preferred_element_type=jnp.float32)
    lifted = jnp.dot(piece, w_shared_up, preferred_element_type=jnp.float32)
    hidden = (jax.nn.silu(gated) * lifted).astype(jnp.bfloat16)
    shared_part = (
        jnp.dot(hidden, w_shared_down, preferred_element_type=jnp.float32)
        .astype(jnp.bfloat16)
        .reshape(dp_size, tok_count, width)
    )
    expert_count = w_router.shape[1]
    planes = lax.axis_size("zc")
    plane = lax.axis_index("zc")
    capacity = 4 * tok_count * TOP // (3 * expert_count)
    depth = (planes - 1) * capacity
    slots = dp_size * depth
    mixed_g = lax.all_gather(mixed, "zc", axis=0, tiled=True)
    mixed_g, shared_part = lax.optimization_barrier((mixed_g, shared_part))
    routes_rel = ring_gather(routes[0], "zc")
    routes_g = jnp.take(routes_rel, (plane - jnp.arange(planes, dtype=jnp.int32)) % planes, axis=0)
    routes_g = routes_g.reshape(planes * tok_count, TOP)
    rows_g = mixed_g.shape[0]
    labels = jnp.arange(expert_count, dtype=jnp.int32)
    logits = jnp.dot(mixed_g, w_router, preferred_element_type=jnp.float32)
    chosen = jnp.sum(
        jnp.where(routes_g[:, :, None] == labels[None, None, :], logits[:, None, :], 0.0), axis=2
    )
    highest = jnp.max(chosen, axis=1, keepdims=True)
    expo = jnp.exp(chosen - highest)
    gates = expo / jnp.sum(expo, axis=1, keepdims=True)
    route_flat = routes_g.reshape(-1)
    block_of = (jnp.arange(rows_g * TOP, dtype=jnp.int32) // TOP) // tok_count
    inside = ((route_flat % planes) == plane) & (block_of != plane)
    dest = (route_flat // planes - me_dp) % dp_size
    onehot = ((dest[:, None] == jnp.arange(dp_size, dtype=jnp.int32)[None, :]) & inside[:, None]).astype(jnp.int32)
    slot = jnp.sum(jnp.cumsum(onehot, axis=0) * onehot, axis=1) - 1
    target = jnp.where(inside, dest * depth + slot, -1).reshape(rows_g, TOP)
    hit = target[:, :, None] == jnp.arange(slots, dtype=jnp.int32)[None, None, :]
    placed = jnp.any(hit, axis=1).astype(jnp.bfloat16)
    send = lax.dot_general(
        placed, mixed_g, (((0,), (0,)), ((), ())), preferred_element_type=jnp.float32
    ).astype(jnp.bfloat16)
    recv = ring_out(send.reshape(dp_size, depth, width), "dp")
    rows_p = piece.shape[0]
    routes_p = tags[:, :, :TOP].reshape(rows_p, TOP)
    logits_p = jnp.dot(piece, w_router, preferred_element_type=jnp.float32)
    chosen_p = jnp.sum(
        jnp.where(routes_p[:, :, None] == labels[None, None, :], logits_p[:, None, :], 0.0), axis=2
    )
    expo_p = jnp.exp(chosen_p - jnp.max(chosen_p, axis=1, keepdims=True))
    gates_p = expo_p / jnp.sum(expo_p, axis=1, keepdims=True)
    local_depth = dp_size * capacity
    own_p = (routes_p.reshape(-1) == me_dp * planes + plane).astype(jnp.int32)
    target_p = jnp.where(own_p > 0, jnp.cumsum(own_p) - 1, -1).reshape(rows_p, TOP)
    hit_p = target_p[:, :, None] == jnp.arange(local_depth, dtype=jnp.int32)[None, None, :]
    local_rows = lax.dot_general(
        jnp.any(hit_p, axis=1).astype(jnp.bfloat16),
        piece,
        (((0,), (0,)), ((), ())),
        preferred_element_type=jnp.float32,
    ).astype(jnp.bfloat16)
    mine = jnp.concatenate([recv.reshape(slots, width), local_rows], axis=0)
    swap = [(0, 1), (1, 0)]
    other = lax.ppermute(mine, "core", swap)
    half_rows = expert_rows(
        jnp.concatenate([mine, other], axis=0), w_expert_gate, w_expert_up, w_expert_down
    )
    held = slots + local_depth
    from_partner = lax.ppermute(half_rows[held:], "core", swap)
    expert_all = (
        half_rows[:held].astype(jnp.float32) + from_partner.astype(jnp.float32)
    ).astype(jnp.bfloat16)
    expert_out = expert_all[:slots]
    back = ring_back(expert_out.reshape(dp_size, depth, width), "dp").reshape(slots, width)
    comb_p = jnp.sum(jnp.where(hit_p, gates_p[:, :, None], 0.0), axis=1)
    first_p = comb_p.astype(jnp.bfloat16)
    rest_p = comb_p - first_p.astype(jnp.float32)
    second_p = rest_p.astype(jnp.bfloat16)
    third_p = (rest_p - second_p.astype(jnp.float32)).astype(jnp.bfloat16)
    local_out = expert_all[slots:]
    routed_p = (
        jnp.dot(first_p, local_out, preferred_element_type=jnp.float32)
        + jnp.dot(second_p, local_out, preferred_element_type=jnp.float32)
        + jnp.dot(third_p, local_out, preferred_element_type=jnp.float32)
    )
    shared_send = (
        shared_part.astype(jnp.float32) + routed_p.reshape(dp_size, tok_count, width)
    ).astype(jnp.bfloat16)
    comb = jnp.sum(jnp.where(hit, gates[:, :, None], 0.0), axis=1)
    first = comb.astype(jnp.bfloat16)
    rest = comb - first.astype(jnp.float32)
    second = rest.astype(jnp.bfloat16)
    third = (rest - second.astype(jnp.float32)).astype(jnp.bfloat16)
    partial = (
        jnp.dot(first, back, preferred_element_type=jnp.float32)
        + jnp.dot(second, back, preferred_element_type=jnp.float32)
        + jnp.dot(third, back, preferred_element_type=jnp.float32)
    )
    routed = lax.psum_scatter(
        partial.astype(jnp.bfloat16), "zc", scatter_dimension=0, tiled=True
    ).astype(jnp.float32)
    shared_sum = ring_scatter(shared_send, "dp")
    output = (residual.astype(jnp.float32) + shared_sum + routed).astype(jnp.bfloat16)
    return output[None]


def solution(mesh):
    dp_size = mesh.shape["dp"]
    planes = mesh.shape["expert"] // 2
    fine = jax.sharding.Mesh(mesh.devices.reshape(dp_size, planes, 2), ("dp", "zc", "core"))
    ex = ("zc", "core")
    in_specs = (
        P(ex, "dp", None),
        P(ex, "dp"),
        P(ex, "dp", None),
        P(),
        P(None, "dp"),
        P(None, "dp"),
        P(None, "dp"),
        P("dp", None),
        P(),
        P(),
        P(None, "dp"),
        P(None, "dp"),
        P("dp", None),
        P(None, ("dp",) + ex),
        P(None, ("dp",) + ex),
        P(("dp",) + ex, None),
    )
    out_specs = P(ex, "dp", None)
    return jax.shard_map(
        per_device, mesh=fine, in_specs=in_specs, out_specs=out_specs, check_vma=False
    )
```
